256 devices in a mesh: clu: 32 (over x, z), grp: 8 (over y, core).
Axes of the slice: x: 4, y: 4, z: 8, core: 2. Of those that a mesh axis runs over, the one named last changes fastest.
Arguments:
- tokens: bfloat16 [262144, 1024], P(('clu', 'grp')), may hold values from -6 to 6
- segment_ids: int32 [256, 1024], P(('clu', 'grp')), may hold values from 0 to 127, never falling along the last dimension, each value on 1 to 32 neighbouring positions
- w_in: bfloat16 [1024, 2048], replicated, may hold values from -0.1875 to 0.1875
- b_in: float32 [2048], replicated, may hold values from -4 to 4
- w_out: bfloat16 [2048, 1024], replicated, may hold values from -0.125 to 0.125
- b_out: float32 [1024], replicated, may hold values from -1.5 to 1.5
- owner_ids: int32 [32768, 1], P(('clu', 'grp')), may hold values from 0 to 31; in each aligned block of 128 rows (0 to 127, 128 to 255, ...) at most 8 rows name the same one
- sub_ids: int32 [32768], P(('clu', 'grp')), may hold values from 0 to 511
Outputs:
- pooled: bfloat16 [32768, 1024], P(('clu', 'grp'))
- nearest: float32 [32768], P(('clu', 'grp'))
The draws below stay inside these ranges and needn't reach their ends.
Inputs may be any that keep to these rules, and one draw needn't show every extreme that they name: `owner_ids`: no device holds more than 8 documents of one owner; some device holds exactly 8. `segment_ids`: each row lists documents 0 to 127 in order, each on 1 to 32 consecutive positions, one on exactly 32.
All inputs are finite; a program needn't handle non-finite values.
Results may differ from the reference program's by a relative error of at most 0.0043.
Values may be sent and summed in bfloat16 or wider, within the bound.
No kernel may reach another device: no remote copies, remote signals or barrier semaphores. Data moves between devices by JAX's collectives and lax.ppermute only.
A program may use at most 64 MiB of HBM per device.

```python
import math
import jax
import jax.numpy as jnp
import numpy as np
from jax import lax

D = 1024
FF = 2048
MOST_LEN = 32
TOK_DEV = 1024
DOCS_DEV = 128
SUBS = 512
CAP = 8
TOKENS = 262144
DOCS = 32768
N_CLU = 32
DEVICES = 256


def touch_ends(result, stream_key, low, largest):
    place = [jax.random.randint(jax.random.fold_in(stream_key, axis), (), 0, length) for axis, length in enumerate(result.shape)]
    widest = result.shape.index(max(result.shape))
    next_to = place[:widest] + [(place[widest] + 1) % result.shape[widest]] + place[widest + 1:]
    return result.at[tuple(place)].set(low).at[tuple(next_to)].set(largest)


def shard_levels(rng, extent, cuts, low, high):
    def one(axis_at, parts):
        steps = jax.random.uniform(jax.random.fold_in(jax.random.fold_in(rng, 6), axis_at), (parts,), jnp.float32, low / len(cuts), high / len(cuts))
        return jnp.repeat(jnp.exp(steps), extent[axis_at] // parts).reshape((-1,) + (1,) * (len(extent) - axis_at - 1))

    gain = one(*cuts[0])
    for cut in cuts[1:]:
        gain = gain * one(*cut)
    return gain


def length_profile(number_of, total, bound, lean):
    portions = [(1 << 20) // math.isqrt(standing ** lean) + 1 for standing in range(2, number_of + 1)]
    rest, holding = total - bound - (number_of - 1), [1] * (number_of - 1)
    while rest > 0:
        free = [i for i in range(number_of - 1) if holding[i] < bound]
        whole, budget = sum([portions[i] for i in free]), rest
        for i in free:
            addition = min(bound - holding[i], max(1, budget * portions[i] // whole), rest)
            holding[i] = holding[i] + addition
            rest = rest - addition
    return np.array([bound] + holding)


def ragged_sizes(stream_key, amount, total, most, slope):
    if amount == 2:
        one = jax.random.randint(stream_key, (), max(1, total - most), min(most, total - 1) + 1)
        return jnp.stack([one, total - one])
    lengths = jnp.asarray(length_profile(amount, total, most, slope), jnp.int32)
    couples = (amount - 1) // 2
    giver, sink = lengths[1:1 + 2 * couples:2], lengths[2:2 + 2 * couples:2]
    room = jnp.minimum(giver - 1, most - sink)
    shifted = jax.random.randint(jax.random.fold_in(stream_key, 1), (couples,), 0, 1 << 20) % (room + 1)
    lengths = lengths.at[1:1 + 2 * couples:2].set(giver - shifted).at[2:2 + 2 * couples:2].set(sink + shifted)
    return lengths[jax.random.permutation(jax.random.fold_in(stream_key, 2), amount)]


def assign_block(rng, own, number, rows, number_of, top, limit, skew):
    order = jax.random.permutation(rng, number_of)
    heavy_load, usual = shares(number_of, rows * top, limit, skew, True), shares(number_of, rows * top, limit, skew, False)
    places = jnp.arange(number_of)

    def named(lengths, offset_by):
        used = int((lengths > 0).sum())
        fixed = max(1, used // 4)
        shifted = fixed + (places - fixed + offset_by * (used - fixed)) % max(1, number_of - fixed)
        return jnp.zeros((number_of,), jnp.int32).at[order[jnp.where(places < fixed, places, shifted)]].set(jnp.asarray(lengths, jnp.int32))

    lengths = jnp.where(number % 4 == 0, named(heavy_load, number // 4), named(usual, number - number // 4 - 1))
    mixed = jax.random.permutation(jax.random.fold_in(own, 3), number_of)
    donor, receiver = mixed[0:number_of // 2 * 2:2], mixed[1:number_of // 2 * 2:2]
    slack = jnp.minimum(lengths[donor] - 1, limit - lengths[receiver]) // 2
    slack = jnp.where((donor == order[0]) | (receiver == order[0]) | (lengths[receiver] == 0), 0, jnp.maximum(slack, 0))
    shifted = jax.random.randint(jax.random.fold_in(own, 4), (number_of // 2,), 0, 1 << 20) % (slack + 1)
    lengths = lengths.at[donor].add(-shifted).at[receiver].add(shifted)
    labels = jnp.searchsorted(jnp.cumsum(lengths), jnp.arange(rows * top), side="right").astype(jnp.int32)
    grid = labels.reshape(top, rows).T
    grid = grid[jax.random.permutation(jax.random.fold_in(own, 1), rows)]
    offset_by = jax.random.randint(jax.random.fold_in(own, 2), (rows, 1), 0, top)
    return jnp.take_along_axis(grid, (jnp.arange(top)[None, :] + offset_by) % top, axis=1)


def shares(number_of, total, reach, slope, full):
    portions = [(1 << 20) // math.isqrt(grade ** slope) + 1 for grade in range(1, number_of + 1)]
    largest = reach if full else min(reach, max(-(-total // number_of), total * portions[0] // sum(portions)))
    least = 1 if total - largest >= number_of - 1 else 0
    given, spare = [largest] + [least] * (number_of - 1), total - largest - least * (number_of - 1)
    while spare > 0:
        movable = [i for i in range(1, number_of) if given[i] < largest] or [i for i in range(1, number_of) if given[i] < reach]
        mass, remaining = sum([portions[i] for i in movable]), spare
        for i in movable:
            extra = min(reach - given[i], max(1, remaining * portions[i] // mass), spare)
            given[i] = given[i] + extra
            spare = spare - extra
    return np.array(given)


def gaussian(key, shape, spread, most, pieces=(), held_as=jnp.bfloat16):
    entries = spread * jax.random.normal(key, shape, jnp.float32)
    if pieces:
        entries = entries * shard_levels(key, shape, pieces, -0.22, 0.18)
    return jnp.clip(entries, -most, most).astype(held_as)


def setup_inputs(seed: int = 0) -> dict:
    key_list = jax.random.split(jax.random.key(seed), 9)
    tokens = gaussian(key_list[0], (TOKENS, D), 1.0, 6.0, ((0, 256),))
    segment_ids = jax.vmap(lambda own: jnp.searchsorted(jnp.cumsum(ragged_sizes(own, DOCS_DEV, TOK_DEV, MOST_LEN, 2)), jnp.arange(TOK_DEV), side="right"))(jax.random.split(key_list[1], DEVICES)).reshape((DEVICES, TOK_DEV)).astype(jnp.int32)
    w_in = gaussian(key_list[2], (D, FF), D ** -0.5, 0.1875)
    b_in = gaussian(key_list[3], (FF,), 1.0, 4.0, (), jnp.float32)
    w_out = gaussian(key_list[4], (FF, D), FF ** -0.5, 0.125)
    b_out = gaussian(key_list[5], (D,), 0.3, 1.5, (), jnp.float32)
    owner_ids_keys = jax.random.split(jax.random.fold_in(key_list[6], 1), DOCS // DOCS_DEV)
    owner_ids_turns = jax.random.permutation(jax.random.fold_in(key_list[6], 3), DOCS // DOCS_DEV)
    owner_ids = jax.vmap(lambda own, number: assign_block(jax.random.fold_in(key_list[6], 2), own, number, DOCS_DEV, N_CLU, 1, CAP, 2))(owner_ids_keys, owner_ids_turns).reshape((DOCS, 1))
    sub_ids = touch_ends(jax.random.randint(key_list[7], (DOCS,), 0, SUBS), jax.random.fold_in(key_list[7], 1), 0, SUBS - 1).astype(jnp.int32)
    return dict(tokens=tokens, segment_ids=segment_ids, w_in=w_in, b_in=b_in, w_out=w_out, b_out=b_out, owner_ids=owner_ids, sub_ids=sub_ids)


def encode(token_block, segments, w_in, b_in, w_out, b_out, doc_count):
    pre_act = jnp.dot(token_block, w_in, preferred_element_type=jnp.float32) + b_in
    activated = jax.nn.gelu(pre_act, approximate=False).astype(jnp.bfloat16)
    layer_out = (token_block.astype(jnp.float32) + jnp.dot(activated, w_out, preferred_element_type=jnp.float32) + b_out).astype(jnp.bfloat16)
    member = segments[None, :] == jnp.arange(doc_count, dtype=jnp.int32)[:, None]
    totals = jnp.dot(member.astype(jnp.bfloat16), layer_out, preferred_element_type=jnp.float32)
    counts = lax.optimization_barrier(jnp.sum(member.astype(jnp.float32), axis=1, keepdims=True))
    mean_rows = totals / counts
    scale_inv = lax.rsqrt(lax.optimization_barrier(jnp.sum(mean_rows * mean_rows, axis=1, keepdims=True)) + 1e-06)
    return (mean_rows.astype(jnp.bfloat16), (mean_rows * scale_inv).astype(jnp.bfloat16))

def reference(tokens, segment_ids, w_in, b_in, w_out, b_out, owner_ids, sub_ids):
    blocks = tokens.reshape(DEVICES, TOK_DEV, D)

    def one_device(pair):
        return encode(pair[0], pair[1], w_in, b_in, w_out, b_out, DOCS_DEV)
    pooled, unit_rows = lax.map(one_device, (blocks, segment_ids))
    pooled = pooled.reshape(DOCS, D)
    unit_rows = unit_rows.reshape(DOCS, D)
    owner_rank = owner_ids[:, 0]
    row_limit = DEVICES * CAP

    def per_owner(owner_id):
        flags = jnp.where(owner_rank == owner_id, 0, 1).astype(jnp.int32)
        order_index = jnp.argsort(flags, stable=True)[:row_limit].astype(jnp.int32)
        valid_rows = owner_rank[order_index] == owner_id
        chosen = unit_rows[order_index]
        cluster_key = jnp.where(valid_rows, sub_ids[order_index], -1)
        similar = jnp.dot(chosen, chosen.T, preferred_element_type=jnp.float32)
        position = jnp.arange(row_limit, dtype=jnp.int32)
        matched = (cluster_key[:, None] == cluster_key[None, :]) & (cluster_key[:, None] >= 0) & (position[:, None] != position[None, :])
        best_sim = lax.optimization_barrier(jnp.max(jnp.where(matched, similar, -1.0), axis=1))
        return (order_index, jnp.where(valid_rows, best_sim, 0.0))
    orders, bests = lax.map(per_owner, jnp.arange(N_CLU, dtype=jnp.int32))
    nearest = jnp.zeros((DOCS,), jnp.float32).at[orders.reshape(-1)].add(bests.reshape(-1))
    return (pooled, nearest)
```

```python
import jax
import jax.numpy as jnp
from jax import lax
from jax.sharding import PartitionSpec as P


def encode(token_block, segments, w_in, b_in, w_out, b_out, doc_count):
    pre_act = jnp.dot(token_block, w_in, preferred_element_type=jnp.float32) + b_in
    activated = jax.nn.gelu(pre_act, approximate=False).astype(jnp.bfloat16)
    layer_out = (
        token_block.astype(jnp.float32)
        + jnp.dot(activated, w_out, preferred_element_type=jnp.float32)
        + b_out
    ).astype(jnp.bfloat16)
    member = segments[None, :] == jnp.arange(doc_count, dtype=jnp.int32)[:, None]
    totals = jnp.dot(member.astype(jnp.bfloat16), layer_out, preferred_element_type=jnp.float32)
    counts = jnp.sum(member.astype(jnp.float32), axis=1, keepdims=True)
    mean_rows = totals / counts
    scale_inv = lax.rsqrt(jnp.sum(mean_rows * mean_rows, axis=1, keepdims=True) + 1e-06)
    return (mean_rows.astype(jnp.bfloat16), (mean_rows * scale_inv).astype(jnp.bfloat16))


def slot_ranks(owner_rank, n_clu):
    hits = (owner_rank[..., None] == jnp.arange(n_clu, dtype=jnp.int32)).astype(jnp.int32)
    before = jnp.cumsum(hits, axis=-2) - hits
    return jnp.sum(before * hits, axis=-1)


def per_device(tokens, segment_ids, w_in, b_in, w_out, b_out, owner_ids, sub_ids):
    n_clu = lax.axis_size("clu")
    n_grp = lax.axis_size("grp")
    doc_count = owner_ids.shape[0]
    model_width = tokens.shape[1]
    capacity = 8
    clu_index = lax.axis_index("clu")
    grp_index = lax.axis_index("grp")

    pooled, unit_rows = encode(tokens, segment_ids[0], w_in, b_in, w_out, b_out, doc_count)

    owner_rank = owner_ids[:, 0]
    slot_index = slot_ranks(owner_rank, n_clu)
    slot_place = owner_rank * capacity + slot_index
    key_code = sub_ids + 1
    lane = jnp.arange(128, dtype=jnp.int32)[None, :]
    meta_cols = jnp.where(
        lane == 0, key_code[:, None] // 64, jnp.where(lane == 1, key_code[:, None] % 64, 0)
    ).astype(jnp.bfloat16)
    rows = jnp.concatenate([unit_rows, meta_cols], axis=1)
    row_width = rows.shape[1]
    send_pick = (
        slot_place[None, :] == jnp.arange(n_clu * capacity, dtype=jnp.int32)[:, None]
    ).astype(jnp.bfloat16)
    send_rows = jnp.dot(send_pick, rows, preferred_element_type=jnp.float32).astype(jnp.bfloat16)
    own_rows = lax.all_to_all(
        send_rows.reshape(n_clu, capacity, row_width), "clu", split_axis=0, concat_axis=0,
        tiled=True,
    ).reshape(n_clu * capacity, row_width)
    all_rows = lax.all_gather(own_rows, "grp", axis=0, tiled=True)

    n_dev = n_clu * n_grp
    key = (
        all_rows[:, model_width].astype(jnp.int32) * 64
        + all_rows[:, model_width + 1].astype(jnp.int32)
        - 1
    )
    own_key = (
        own_rows[:, model_width].astype(jnp.int32) * 64
        + own_rows[:, model_width + 1].astype(jnp.int32)
        - 1
    )
    own_units = own_rows[:, :model_width]
    all_units = all_rows[:, :model_width]

    similar = lax.dot_general(
        own_units, all_units, (((1,), (1,)), ((), ())), preferred_element_type=jnp.float32
    )
    own_pos = grp_index * (n_clu * capacity) + jnp.arange(n_clu * capacity, dtype=jnp.int32)
    matched = (
        (own_key[:, None] == key[None, :])
        & (own_key[:, None] >= 0)
        & (own_pos[:, None] != jnp.arange(n_dev * capacity, dtype=jnp.int32)[None, :])
    )
    best_sim = jnp.max(jnp.where(matched, similar, -1.0), axis=1)
    returned = lax.all_to_all(
        best_sim.reshape(n_clu, capacity), "clu", split_axis=0, concat_axis=0, tiled=True
    ).reshape(n_clu * capacity)
    nearest = jnp.sum(
        jnp.where(
            slot_place[:, None] == jnp.arange(n_clu * capacity, dtype=jnp.int32)[None, :],
            returned[None, :],
            0.0,
        ),
        axis=1,
    )
    return (pooled, nearest)


def solution(mesh):
    in_specs = (
        P(("clu", "grp"), None),
        P(("clu", "grp"), None),
        P(),
        P(),
        P(),
        P(),
        P(("clu", "grp"), None),
        P(("clu", "grp")),
    )
    out_specs = (P(("clu", "grp"), None), P(("clu", "grp")))
    return jax.shard_map(
        per_device, mesh=mesh, in_specs=in_specs, out_specs=out_specs, check_vma=False
    )
```

```python
import jax
import jax.numpy as jnp
from jax import lax
from jax.sharding import PartitionSpec as P


def encode(token_block, segments, w_in, b_in, w_out, b_out, doc_count):
    pre_act = jnp.dot(token_block, w_in, preferred_element_type=jnp.float32) + b_in
    activated = jax.nn.gelu(pre_act, approximate=False).astype(jnp.bfloat16)
    layer_out = (
        token_block.astype(jnp.float32)
        + jnp.dot(activated, w_out, preferred_element_type=jnp.float32)
        + b_out
    ).astype(jnp.bfloat16)
    member = segments[None, :] == jnp.arange(doc_count, dtype=jnp.int32)[:, None]
    totals = jnp.dot(member.astype(jnp.bfloat16), layer_out, preferred_element_type=jnp.float32)
    counts = jnp.sum(member.astype(jnp.float32), axis=1, keepdims=True)
    mean_rows = totals / counts
    scale_inv = lax.rsqrt(jnp.sum(mean_rows * mean_rows, axis=1, keepdims=True) + 1e-06)
    return (mean_rows.astype(jnp.bfloat16), (mean_rows * scale_inv).astype(jnp.bfloat16))


def slot_ranks(owner_rank, n_clu):
    hits = (owner_rank[..., None] == jnp.arange(n_clu, dtype=jnp.int32)).astype(jnp.int32)
    before = jnp.cumsum(hits, axis=-2) - hits
    return jnp.sum(before * hits, axis=-1)


def gather_grp(block):
    n = lax.axis_size("grp")
    chips = n // 2
    core_swap = [(i, i ^ 1) for i in range(n)]
    ring = [
        (i, ((i // 2 + (1 if i % 2 == 0 else chips - 1)) % chips) * 2 + i % 2) for i in range(n)
    ]
    partner = lax.ppermute(block, "grp", core_swap)
    pair = jnp.concatenate([block, partner], axis=0)
    hop1 = lax.ppermute(pair, "grp", ring)
    hop2 = lax.ppermute(hop1[: block.shape[0]], "grp", ring)
    mine = jnp.concatenate([hop1, hop2], axis=0)
    theirs = lax.ppermute(mine, "grp", core_swap)
    return [block, partner, hop1, hop2, theirs]


def per_device(tokens, segment_ids, w_in, b_in, w_out, b_out, owner_ids, sub_ids):
    n_clu = lax.axis_size("clu")
    n_grp = lax.axis_size("grp")
    doc_count = owner_ids.shape[0]
    model_width = tokens.shape[1]
    capacity = 8
    clu_index = lax.axis_index("clu")
    grp_index = lax.axis_index("grp")

    pooled, unit_rows = encode(tokens, segment_ids[0], w_in, b_in, w_out, b_out, doc_count)

    owner_rank = owner_ids[:, 0]
    slot_index = slot_ranks(owner_rank, n_clu)
    slot_place = owner_rank * capacity + slot_index
    key_code = sub_ids + 1
    lane = jnp.arange(128, dtype=jnp.int32)[None, :]
    meta_cols = jnp.where(
        lane == 0, key_code[:, None] // 64, jnp.where(lane == 1, key_code[:, None] % 64, 0)
    ).astype(jnp.bfloat16)
    rows = jnp.concatenate([unit_rows, meta_cols], axis=1)
    row_width = rows.shape[1]
    send_pick = (
        slot_place[None, :] == jnp.arange(n_clu * capacity, dtype=jnp.int32)[:, None]
    ).astype(jnp.bfloat16)
    send_rows = jnp.dot(send_pick, rows, preferred_element_type=jnp.float32).astype(jnp.bfloat16)
    own_rows = lax.all_to_all(
        send_rows.reshape(n_clu, capacity, row_width), "clu", split_axis=0, concat_axis=0,
        tiled=True,
    ).reshape(n_clu * capacity, row_width)
    pieces = gather_grp(own_rows)

    def key_of(rows):
        return (
            rows[:, model_width].astype(jnp.int32) * 64
            + rows[:, model_width + 1].astype(jnp.int32)
            - 1
        )

    own_key = key_of(own_rows)
    own_units = own_rows[:, :model_width]
    slots = n_clu * capacity
    best_sim = jnp.full((slots,), -1.0, jnp.float32)
    for number, piece in enumerate(pieces):
        similar = lax.dot_general(
            own_units, piece[:, :model_width], (((1,), (1,)), ((), ())),
            preferred_element_type=jnp.float32,
        )
        matched = (own_key[:, None] == key_of(piece)[None, :]) & (own_key[:, None] >= 0)
        if number == 0:
            matched = matched & (
                jnp.arange(slots, dtype=jnp.int32)[:, None]
                != jnp.arange(piece.shape[0], dtype=jnp.int32)[None, :]
            )
        best_sim = jnp.maximum(best_sim, jnp.max(jnp.where(matched, similar, -1.0), axis=1))
    returned = lax.all_to_all(
        best_sim.reshape(n_clu, capacity), "clu", split_axis=0, concat_axis=0, tiled=True
    ).reshape(n_clu * capacity)
    nearest = jnp.sum(
        jnp.where(
            slot_place[:, None] == jnp.arange(n_clu * capacity, dtype=jnp.int32)[None, :],
            returned[None, :],
            0.0,
        ),
        axis=1,
    )
    return (pooled, nearest)


def solution(mesh):
    in_specs = (
        P(("clu", "grp"), None),
        P(("clu", "grp"), None),
        P(),
        P(),
        P(),
        P(),
        P(("clu", "grp"), None),
        P(("clu", "grp")),
    )
    out_specs = (P(("clu", "grp"), None), P(("clu", "grp")))
    return jax.shard_map(
        per_device, mesh=mesh, in_specs=in_specs, out_specs=out_specs, check_vma=False
    )
```

```python
import functools

import jax
import jax.numpy as jnp
from jax import lax
from jax.experimental import pallas as pl
from jax.experimental.pallas import tpu as pltpu
from jax.sharding import PartitionSpec as P


def encode_kernel(chunk, seg_ref, x_ref, wi_ref, bi_ref, wo_ref, bo_ref, tot_ref):
    step = pl.program_id(0)
    x = x_ref[...]
    ff = wi_ref.shape[1]
    acc = None
    for k in range(ff // chunk):
        part = slice(k * chunk, (k + 1) * chunk)
        pre_act = jnp.dot(x, wi_ref[:, part], preferred_element_type=jnp.float32) + bi_ref[:, part]
        activated = (pre_act * 0.5 * (1.0 + lax.erf(pre_act * 0.7071067811865476))).astype(
            jnp.bfloat16
        )
        term = jnp.dot(activated, wo_ref[part, :], preferred_element_type=jnp.float32)
        acc = term if acc is None else acc + term
    layer_out = (x.astype(jnp.float32) + acc + bo_ref[...]).astype(jnp.bfloat16)
    docs = tot_ref.shape[0]
    member = (
        seg_ref[...] == lax.broadcasted_iota(jnp.int32, (docs, seg_ref.shape[1]), 0)
    ).astype(jnp.bfloat16)
    part_totals = jnp.dot(member, layer_out, preferred_element_type=jnp.float32)

    @pl.when(step == 0)
    def _():
        tot_ref[...] = part_totals

    @pl.when(step != 0)
    def _():
        tot_ref[...] += part_totals


def encode(token_block, segments, w_in, b_in, w_out, b_out, doc_count):
    rows, width = token_block.shape
    ff = w_in.shape[1]
    tile = 512
    flops = 4 * rows * width * ff + 2 * doc_count * rows * width
    totals = pl.pallas_call(
        functools.partial(encode_kernel, 1024),
        out_shape=jax.ShapeDtypeStruct((doc_count, width), jnp.float32),
        grid=(rows // tile,),
        in_specs=[
            pl.BlockSpec((1, tile), lambda i: (0, i)),
            pl.BlockSpec((tile, width), lambda i: (i, 0)),
            pl.BlockSpec((width, ff), lambda i: (0, 0)),
            pl.BlockSpec((1, ff), lambda i: (0, 0)),
            pl.BlockSpec((ff, width), lambda i: (0, 0)),
            pl.BlockSpec((1, width), lambda i: (0, 0)),
        ],
        out_specs=pl.BlockSpec((doc_count, width), lambda i: (0, 0)),
        compiler_params=pltpu.CompilerParams(
            dimension_semantics=("arbitrary",), vmem_limit_bytes=60 * 1024 * 1024
        ),
        cost_estimate=pl.CostEstimate(
            flops=flops, transcendentals=rows * ff, bytes_accessed=2 * rows * width + 8 * width * ff
        ),
    )(segments.reshape(1, rows), token_block, w_in, b_in.reshape(1, ff), w_out, b_out.reshape(1, width))
    member = segments[None, :] == jnp.arange(doc_count, dtype=jnp.int32)[:, None]
    counts = jnp.sum(member.astype(jnp.float32), axis=1, keepdims=True)
    mean_rows = totals / counts
    scale_inv = lax.rsqrt(jnp.sum(mean_rows * mean_rows, axis=1, keepdims=True) + 1e-06)
    return (mean_rows.astype(jnp.bfloat16), (mean_rows * scale_inv).astype(jnp.bfloat16))


def slot_ranks(owner_rank, n_clu):
    hits = (owner_rank[..., None] == jnp.arange(n_clu, dtype=jnp.int32)).astype(jnp.int32)
    before = jnp.cumsum(hits, axis=-2) - hits
    return jnp.sum(before * hits, axis=-1)


def gather_grp(block):
    n = lax.axis_size("grp")
    chips = n // 2
    core_swap = [(i, i ^ 1) for i in range(n)]
    ring = [
        (i, ((i // 2 + (1 if i % 2 == 0 else chips - 1)) % chips) * 2 + i % 2) for i in range(n)
    ]
    partner = lax.ppermute(block, "grp", core_swap)
    pair = jnp.concatenate([block, partner], axis=0)
    hop1 = lax.ppermute(pair, "grp", ring)
    hop2 = lax.ppermute(hop1[: block.shape[0]], "grp", ring)
    mine = jnp.concatenate([hop1, hop2], axis=0)
    theirs = lax.ppermute(mine, "grp", core_swap)
    return [block, partner, hop1, hop2, theirs]


def per_device(tokens, segment_ids, w_in, b_in, w_out, b_out, owner_ids, sub_ids):
    n_clu = lax.axis_size("clu")
    n_grp = lax.axis_size("grp")
    doc_count = owner_ids.shape[0]
    model_width = tokens.shape[1]
    capacity = 8
    clu_index = lax.axis_index("clu")
    grp_index = lax.axis_index("grp")

    pooled, unit_rows = encode(tokens, segment_ids[0], w_in, b_in, w_out, b_out, doc_count)

    owner_rank = owner_ids[:, 0]
    slot_index = slot_ranks(owner_rank, n_clu)
    slot_place = owner_rank * capacity + slot_index
    key_code = sub_ids + 1
    lane = jnp.arange(128, dtype=jnp.int32)[None, :]
    meta_cols = jnp.where(
        lane == 0, key_code[:, None] // 64, jnp.where(lane == 1, key_code[:, None] % 64, 0)
    ).astype(jnp.bfloat16)
    rows = jnp.concatenate([unit_rows, meta_cols], axis=1)
    row_width = rows.shape[1]
    send_pick = (
        slot_place[None, :] == jnp.arange(n_clu * capacity, dtype=jnp.int32)[:, None]
    ).astype(jnp.bfloat16)
    send_rows = jnp.dot(send_pick, rows, preferred_element_type=jnp.float32).astype(jnp.bfloat16)
    own_rows = lax.all_to_all(
        send_rows.reshape(n_clu, capacity, row_width), "clu", split_axis=0, concat_axis=0,
        tiled=True,
    ).reshape(n_clu * capacity, row_width)
    pieces = gather_grp(own_rows)

    def key_of(rows):
        return (
            rows[:, model_width].astype(jnp.int32) * 64
            + rows[:, model_width + 1].astype(jnp.int32)
            - 1
        )

    own_key = key_of(own_rows)
    own_units = own_rows[:, :model_width]
    slots = n_clu * capacity
    best_sim = jnp.full((slots,), -1.0, jnp.float32)
    for number, piece in enumerate(pieces):
        similar = lax.dot_general(
            own_units, piece[:, :model_width], (((1,), (1,)), ((), ())),
            preferred_element_type=jnp.float32,
        )
        matched = (own_key[:, None] == key_of(piece)[None, :]) & (own_key[:, None] >= 0)
        if number == 0:
            matched = matched & (
                jnp.arange(slots, dtype=jnp.int32)[:, None]
                != jnp.arange(piece.shape[0], dtype=jnp.int32)[None, :]
            )
        best_sim = jnp.maximum(best_sim, jnp.max(jnp.where(matched, similar, -1.0), axis=1))
    returned = lax.all_to_all(
        best_sim.reshape(n_clu, capacity), "clu", split_axis=0, concat_axis=0, tiled=True
    ).reshape(n_clu * capacity)
    nearest = jnp.sum(
        jnp.where(
            slot_place[:, None] == jnp.arange(n_clu * capacity, dtype=jnp.int32)[None, :],
            returned[None, :],
            0.0,
        ),
        axis=1,
    )
    return (pooled, nearest)


def solution(mesh):
    in_specs = (
        P(("clu", "grp"), None),
        P(("clu", "grp"), None),
        P(),
        P(),
        P(),
        P(),
        P(("clu", "grp"), None),
        P(("clu", "grp")),
    )
    out_specs = (P(("clu", "grp"), None), P(("clu", "grp")))
    return jax.shard_map(
        per_device, mesh=mesh, in_specs=in_specs, out_specs=out_specs, check_vma=False
    )
```

```python
import functools

import jax
import jax.numpy as jnp
from jax import lax
from jax.experimental import pallas as pl
from jax.experimental.pallas import tpu as pltpu
from jax.sharding import PartitionSpec as P


def encode_kernel(chunk, seg_ref, x_ref, wi_ref, bi_ref, wo_ref, bo_ref, tot_ref):
    step = pl.program_id(0)
    x = x_ref[...]
    ff = wi_ref.shape[1]
    acc = None
    for k in range(ff // chunk):
        part = slice(k * chunk, (k + 1) * chunk)
        pre_act = jnp.dot(x, wi_ref[:, part], preferred_element_type=jnp.float32) + bi_ref[:, part]
        activated = (pre_act * 0.5 * (1.0 + lax.erf(pre_act * 0.7071067811865476))).astype(
            jnp.bfloat16
        )
        term = jnp.dot(activated, wo_ref[part, :], preferred_element_type=jnp.float32)
        acc = term if acc is None else acc + term
    layer_out = (x.astype(jnp.float32) + acc + bo_ref[...]).astype(jnp.bfloat16)
    docs = tot_ref.shape[0]
    member = (
        seg_ref[...] == lax.broadcasted_iota(jnp.int32, (docs, seg_ref.shape[1]), 0)
    ).astype(jnp.bfloat16)
    part_totals = jnp.dot(member, layer_out, preferred_element_type=jnp.float32)

    @pl.when(step == 0)
    def _():
        tot_ref[...] = part_totals

    @pl.when(step != 0)
    def _():
        tot_ref[...] += part_totals


def encode(token_block, segments, w_in, b_in, w_out, b_out, doc_count):
    rows, width = token_block.shape
    ff = w_in.shape[1]
    tile = 512
    flops = 4 * rows * width * ff + 2 * doc_count * rows * width
    totals = pl.pallas_call(
        functools.partial(encode_kernel, 1024),
        out_shape=jax.ShapeDtypeStruct((doc_count, width), jnp.float32),
        grid=(rows // tile,),
        in_specs=[
            pl.BlockSpec((1, tile), lambda i: (0, i)),
            pl.BlockSpec((tile, width), lambda i: (i, 0)),
            pl.BlockSpec((width, ff), lambda i: (0, 0)),
            pl.BlockSpec((1, ff), lambda i: (0, 0)),
            pl.BlockSpec((ff, width), lambda i: (0, 0)),
            pl.BlockSpec((1, width), lambda i: (0, 0)),
        ],
        out_specs=pl.BlockSpec((doc_count, width), lambda i: (0, 0)),
        compiler_params=pltpu.CompilerParams(
            dimension_semantics=("arbitrary",), vmem_limit_bytes=60 * 1024 * 1024
        ),
        cost_estimate=pl.CostEstimate(
            flops=flops, transcendentals=rows * ff, bytes_accessed=2 * rows * width + 8 * width * ff
        ),
    )(segments.reshape(1, rows), token_block, w_in, b_in.reshape(1, ff), w_out, b_out.reshape(1, width))
    member = segments[None, :] == jnp.arange(doc_count, dtype=jnp.int32)[:, None]
    counts = jnp.sum(member.astype(jnp.float32), axis=1, keepdims=True)
    mean_rows = totals / counts
    scale_inv = lax.rsqrt(jnp.sum(mean_rows * mean_rows, axis=1, keepdims=True) + 1e-06)
    return (mean_rows.astype(jnp.bfloat16), (mean_rows * scale_inv).astype(jnp.bfloat16))


def slot_ranks(owner_rank, n_clu):
    hits = (owner_rank[..., None] == jnp.arange(n_clu, dtype=jnp.int32)).astype(jnp.int32)
    before = jnp.cumsum(hits, axis=-2) - hits
    return jnp.sum(before * hits, axis=-1)


def gather_grp(block):
    n = lax.axis_size("grp")
    chips = n // 2
    core_swap = [(i, i ^ 1) for i in range(n)]
    ring = [
        (i, ((i // 2 + (1 if i % 2 == 0 else chips - 1)) % chips) * 2 + i % 2) for i in range(n)
    ]
    near = lax.ppermute(block, "grp", ring)
    partner = lax.ppermute(block, "grp", core_swap)
    near_partner = lax.ppermute(partner, "grp", ring)
    far = lax.ppermute(near, "grp", ring)
    swapped = [lax.ppermute(piece, "grp", core_swap) for piece in (near, near_partner, far)]
    return [block, partner, near, near_partner, far] + swapped


def per_device(tokens, segment_ids, w_in, b_in, w_out, b_out, owner_ids, sub_ids):
    n_clu = lax.axis_size("clu")
    n_grp = lax.axis_size("grp")
    doc_count = owner_ids.shape[0]
    model_width = tokens.shape[1]
    capacity = 8
    clu_index = lax.axis_index("clu")
    grp_index = lax.axis_index("grp")

    pooled, unit_rows = encode(tokens, segment_ids[0], w_in, b_in, w_out, b_out, doc_count)

    owner_rank = owner_ids[:, 0]
    slot_index = slot_ranks(owner_rank, n_clu)
    slot_place = owner_rank * capacity + slot_index
    key_code = sub_ids + 1
    lane = jnp.arange(128, dtype=jnp.int32)[None, :]
    meta_cols = jnp.where(
        lane == 0, key_code[:, None] // 64, jnp.where(lane == 1, key_code[:, None] % 64, 0)
    ).astype(jnp.bfloat16)
    rows = jnp.concatenate([unit_rows, meta_cols], axis=1)
    row_width = rows.shape[1]
    send_pick = (
        slot_place[None, :] == jnp.arange(n_clu * capacity, dtype=jnp.int32)[:, None]
    ).astype(jnp.bfloat16)
    send_rows = jnp.dot(send_pick, rows, preferred_element_type=jnp.float32).astype(jnp.bfloat16)
    own_rows = lax.all_to_all(
        send_rows.reshape(n_clu, capacity, row_width), "clu", split_axis=0, concat_axis=0,
        tiled=True,
    ).reshape(n_clu * capacity, row_width)
    pieces = gather_grp(own_rows)

    def key_of(rows):
        return (
            rows[:, model_width].astype(jnp.int32) * 64
            + rows[:, model_width + 1].astype(jnp.int32)
            - 1
        )

    own_key = key_of(own_rows)
    own_units = own_rows[:, :model_width]
    slots = n_clu * capacity
    best_sim = jnp.full((slots,), -1.0, jnp.float32)
    for number, piece in enumerate(pieces):
        similar = lax.dot_general(
            own_units, piece[:, :model_width], (((1,), (1,)), ((), ())),
            preferred_element_type=jnp.float32,
        )
        matched = (own_key[:, None] == key_of(piece)[None, :]) & (own_key[:, None] >= 0)
        if number == 0:
            matched = matched & (
                jnp.arange(slots, dtype=jnp.int32)[:, None]
                != jnp.arange(piece.shape[0], dtype=jnp.int32)[None, :]
            )
        best_sim = jnp.maximum(best_sim, jnp.max(jnp.where(matched, similar, -1.0), axis=1))
    returned = lax.all_to_all(
        best_sim.reshape(n_clu, capacity), "clu", split_axis=0, concat_axis=0, tiled=True
    ).reshape(n_clu * capacity)
    nearest = jnp.sum(
        jnp.where(
            slot_place[:, None] == jnp.arange(n_clu * capacity, dtype=jnp.int32)[None, :],
            returned[None, :],
            0.0,
        ),
        axis=1,
    )
    return (pooled, nearest)


def solution(mesh):
    in_specs = (
        P(("clu", "grp"), None),
        P(("clu", "grp"), None),
        P(),
        P(),
        P(),
        P(),
        P(("clu", "grp"), None),
        P(("clu", "grp")),
    )
    out_specs = (P(("clu", "grp"), None), P(("clu", "grp")))
    return jax.shard_map(
        per_device, mesh=mesh, in_specs=in_specs, out_specs=out_specs, check_vma=False
    )
```

```python
import functools

import jax
import jax.numpy as jnp
from jax import lax
from jax.experimental import pallas as pl
from jax.experimental.pallas import tpu as pltpu
from jax.sharding import PartitionSpec as P


def encode_kernel(chunk, seg_ref, x_ref, wi_ref, bi_ref, wo_ref, bo_ref, tot_ref):
    step = pl.program_id(0)
    x = x_ref[...]
    ff = wi_ref.shape[1]
    acc = None
    for k in range(ff // chunk):
        part = slice(k * chunk, (k + 1) * chunk)
        pre_act = jnp.dot(x, wi_ref[:, part], preferred_element_type=jnp.float32) + bi_ref[:, part]
        activated = (pre_act * 0.5 * (1.0 + lax.erf(pre_act * 0.7071067811865476))).astype(
            jnp.bfloat16
        )
        term = jnp.dot(activated, wo_ref[part, :], preferred_element_type=jnp.float32)
        acc = term if acc is None else acc + term
    layer_out = (x.astype(jnp.float32) + acc + bo_ref[...]).astype(jnp.bfloat16)
    docs = tot_ref.shape[0]
    member = (
        seg_ref[...] == lax.broadcasted_iota(jnp.int32, (docs, seg_ref.shape[1]), 0)
    ).astype(jnp.bfloat16)
    part_totals = jnp.dot(member, layer_out, preferred_element_type=jnp.float32)

    @pl.when(step == 0)
    def _():
        tot_ref[...] = part_totals

    @pl.when(step != 0)
    def _():
        tot_ref[...] += part_totals


def encode(token_block, segments, w_in, b_in, w_out, b_out, doc_count):
    rows, width = token_block.shape
    ff = w_in.shape[1]
    tile = 512
    flops = 4 * rows * width * ff + 2 * doc_count * rows * width
    totals = pl.pallas_call(
        functools.partial(encode_kernel, 1024),
        out_shape=jax.ShapeDtypeStruct((doc_count, width), jnp.float32),
        grid=(rows // tile,),
        in_specs=[
            pl.BlockSpec((1, tile), lambda i: (0, i)),
            pl.BlockSpec((tile, width), lambda i: (i, 0)),
            pl.BlockSpec((width, ff), lambda i: (0, 0)),
            pl.BlockSpec((1, ff), lambda i: (0, 0)),
            pl.BlockSpec((ff, width), lambda i: (0, 0)),
            pl.BlockSpec((1, width), lambda i: (0, 0)),
        ],
        out_specs=pl.BlockSpec((doc_count, width), lambda i: (0, 0)),
        compiler_params=pltpu.CompilerParams(
            dimension_semantics=("arbitrary",), vmem_limit_bytes=60 * 1024 * 1024
        ),
        cost_estimate=pl.CostEstimate(
            flops=flops, transcendentals=rows * ff, bytes_accessed=2 * rows * width + 8 * width * ff
        ),
    )(segments.reshape(1, rows), token_block, w_in, b_in.reshape(1, ff), w_out, b_out.reshape(1, width))
    return totals


def epilogue_kernel(
    capacity, n_owner, seg_ref, tot_ref, own_ref, sub_ref, pooled_ref, send_ref, place_ref
):
    docs, width = tot_ref.shape
    positions = seg_ref.shape[1]
    member = seg_ref[...] == lax.broadcasted_iota(jnp.int32, (docs, positions), 0)
    counts = jnp.sum(member.astype(jnp.float32), axis=1, keepdims=True)
    mean_rows = tot_ref[...] / counts
    pooled_ref[...] = mean_rows.astype(jnp.bfloat16)
    scale_inv = lax.rsqrt(jnp.sum(mean_rows * mean_rows, axis=1, keepdims=True) + 1e-06)
    unit_rows = (mean_rows * scale_inv).astype(jnp.bfloat16)
    owner = own_ref[...]
    hits = (owner == lax.broadcasted_iota(jnp.int32, (docs, n_owner), 1)).astype(jnp.bfloat16)
    lower = (
        lax.broadcasted_iota(jnp.int32, (docs, docs), 1)
        < lax.broadcasted_iota(jnp.int32, (docs, docs), 0)
    ).astype(jnp.bfloat16)
    before = jnp.dot(lower, hits, preferred_element_type=jnp.float32)
    rank = jnp.sum(before * hits.astype(jnp.float32), axis=1, keepdims=True).astype(jnp.int32)
    place = owner * capacity + rank
    diagonal = lax.broadcasted_iota(jnp.int32, (docs, docs), 0) == lax.broadcasted_iota(
        jnp.int32, (docs, docs), 1
    )
    place_row = jnp.sum(jnp.where(diagonal, place, 0), axis=0, keepdims=True)
    place_ref[...] = place_row
    slots = send_ref.shape[0]
    pick = (place_row == lax.broadcasted_iota(jnp.int32, (slots, docs), 0)).astype(jnp.bfloat16)
    send_ref[:, :width] = jnp.dot(pick, unit_rows, preferred_element_type=jnp.float32).astype(
        jnp.bfloat16
    )
    key_code = sub_ref[...] + 1
    lane = lax.broadcasted_iota(jnp.int32, (docs, send_ref.shape[1] - width), 1)
    meta_cols = jnp.where(
        lane == 0, key_code // 64, jnp.where(lane == 1, key_code % 64, 0)
    ).astype(jnp.bfloat16)
    send_ref[:, width:] = jnp.dot(pick, meta_cols, preferred_element_type=jnp.float32).astype(
        jnp.bfloat16
    )


def epilogue(segments, totals, owner_ids, sub_ids, capacity, n_owner):
    docs, width = totals.shape
    slots = n_owner * capacity
    vmem = pl.BlockSpec(memory_space=pltpu.VMEM)
    return pl.pallas_call(
        functools.partial(epilogue_kernel, capacity, n_owner),
        out_shape=(
            jax.ShapeDtypeStruct((docs, width), jnp.bfloat16),
            jax.ShapeDtypeStruct((slots, width + 128), jnp.bfloat16),
            jax.ShapeDtypeStruct((1, docs), jnp.int32),
        ),
        in_specs=[vmem] * 4,
        out_specs=(vmem, vmem, vmem),
        cost_estimate=pl.CostEstimate(
            flops=2 * slots * docs * (width + 128), transcendentals=docs,
            bytes_accessed=4 * docs * width + 2 * docs * width + 2 * slots * (width + 128),
        ),
    )(segments.reshape(1, -1), totals, owner_ids, sub_ids.reshape(docs, 1))


def gather_grp(block):
    n = lax.axis_size("grp")
    chips = n // 2
    core_swap = [(i, i ^ 1) for i in range(n)]
    ring = [
        (i, ((i // 2 + (1 if i % 2 == 0 else chips - 1)) % chips) * 2 + i % 2) for i in range(n)
    ]
    near = lax.ppermute(block, "grp", ring)
    partner = lax.ppermute(block, "grp", core_swap)
    near_partner = lax.ppermute(partner, "grp", ring)
    far = lax.ppermute(near, "grp", ring)
    swapped = [lax.ppermute(piece, "grp", core_swap) for piece in (near, near_partner, far)]
    return [block, partner, near, near_partner, far] + swapped


def per_device(tokens, segment_ids, w_in, b_in, w_out, b_out, owner_ids, sub_ids):
    n_clu = lax.axis_size("clu")
    n_grp = lax.axis_size("grp")
    doc_count = owner_ids.shape[0]
    model_width = tokens.shape[1]
    capacity = 8
    clu_index = lax.axis_index("clu")
    grp_index = lax.axis_index("grp")

    totals = encode(tokens, segment_ids[0], w_in, b_in, w_out, b_out, doc_count)
    pooled, send_rows, place_row = epilogue(
        segment_ids[0], totals, owner_ids, sub_ids, capacity, n_clu
    )
    slot_place = place_row[0]
    row_width = send_rows.shape[1]
    own_rows = lax.all_to_all(
        send_rows.reshape(n_clu, capacity, row_width), "clu", split_axis=0, concat_axis=0,
        tiled=True,
    ).reshape(n_clu * capacity, row_width)
    pieces = gather_grp(own_rows)

    def key_of(rows):
        return (
            rows[:, model_width].astype(jnp.int32) * 64
            + rows[:, model_width + 1].astype(jnp.int32)
            - 1
        )

    own_key = key_of(own_rows)
    own_units = own_rows[:, :model_width]
    slots = n_clu * capacity
    best_sim = jnp.full((slots,), -1.0, jnp.float32)
    for number, piece in enumerate(pieces):
        similar = lax.dot_general(
            own_units, piece[:, :model_width], (((1,), (1,)), ((), ())),
            preferred_element_type=jnp.float32,
        )
        matched = (own_key[:, None] == key_of(piece)[None, :]) & (own_key[:, None] >= 0)
        if number == 0:
            matched = matched & (
                jnp.arange(slots, dtype=jnp.int32)[:, None]
                != jnp.arange(piece.shape[0], dtype=jnp.int32)[None, :]
            )
        best_sim = jnp.maximum(best_sim, jnp.max(jnp.where(matched, similar, -1.0), axis=1))
    returned = lax.all_to_all(
        best_sim.reshape(n_clu, capacity), "clu", split_axis=0, concat_axis=0, tiled=True
    ).reshape(n_clu * capacity)
    nearest = jnp.sum(
        jnp.where(
            slot_place[:, None] == jnp.arange(n_clu * capacity, dtype=jnp.int32)[None, :],
            returned[None, :],
            0.0,
        ),
        axis=1,
    )
    return (pooled, nearest)


def solution(mesh):
    in_specs = (
        P(("clu", "grp"), None),
        P(("clu", "grp"), None),
        P(),
        P(),
        P(),
        P(),
        P(("clu", "grp"), None),
        P(("clu", "grp")),
    )
    out_specs = (P(("clu", "grp"), None), P(("clu", "grp")))
    return jax.shard_map(
        per_device, mesh=mesh, in_specs=in_specs, out_specs=out_specs, check_vma=False
    )
```

```python
import functools

import jax
import jax.numpy as jnp
from jax import lax
from jax.experimental import pallas as pl
from jax.experimental.pallas import tpu as pltpu
from jax.sharding import PartitionSpec as P


def encode_kernel(chunk, seg_ref, x_ref, wi_ref, bi_ref, wo_ref, bo_ref, tot_ref):
    step = pl.program_id(0)
    x = x_ref[...]
    ff = wi_ref.shape[1]
    acc = None
    for k in range(ff // chunk):
        part = slice(k * chunk, (k + 1) * chunk)
        pre_act = jnp.dot(x, wi_ref[:, part], preferred_element_type=jnp.float32) + bi_ref[:, part]
        activated = (pre_act * 0.5 * (1.0 + lax.erf(pre_act * 0.7071067811865476))).astype(
            jnp.bfloat16
        )
        term = jnp.dot(activated, wo_ref[part, :], preferred_element_type=jnp.float32)
        acc = term if acc is None else acc + term
    layer_out = (x.astype(jnp.float32) + acc + bo_ref[...]).astype(jnp.bfloat16)
    docs = tot_ref.shape[0]
    member = (
        seg_ref[...] == lax.broadcasted_iota(jnp.int32, (docs, seg_ref.shape[1]), 0)
    ).astype(jnp.bfloat16)
    part_totals = jnp.dot(member, layer_out, preferred_element_type=jnp.float32)

    @pl.when(step == 0)
    def _():
        tot_ref[...] = part_totals

    @pl.when(step != 0)
    def _():
        tot_ref[...] += part_totals


def encode(token_block, segments, w_in, b_in, w_out, b_out, doc_count):
    rows, width = token_block.shape
    ff = w_in.shape[1]
    tile = 512
    flops = 4 * rows * width * ff + 2 * doc_count * rows * width
    totals = pl.pallas_call(
        functools.partial(encode_kernel, 1024),
        out_shape=jax.ShapeDtypeStruct((doc_count, width), jnp.float32),
        grid=(rows // tile,),
        in_specs=[
            pl.BlockSpec((1, tile), lambda i: (0, i)),
            pl.BlockSpec((tile, width), lambda i: (i, 0)),
            pl.BlockSpec((width, ff), lambda i: (0, 0)),
            pl.BlockSpec((1, ff), lambda i: (0, 0)),
            pl.BlockSpec((ff, width), lambda i: (0, 0)),
            pl.BlockSpec((1, width), lambda i: (0, 0)),
        ],
        out_specs=pl.BlockSpec((doc_count, width), lambda i: (0, 0)),
        compiler_params=pltpu.CompilerParams(
            dimension_semantics=("arbitrary",), vmem_limit_bytes=60 * 1024 * 1024
        ),
        cost_estimate=pl.CostEstimate(
            flops=flops, transcendentals=rows * ff, bytes_accessed=2 * rows * width + 8 * width * ff
        ),
    )(segments.reshape(1, rows), token_block, w_in, b_in.reshape(1, ff), w_out, b_out.reshape(1, width))
    return totals


def epilogue_kernel(
    capacity, n_owner, seg_ref, tot_ref, own_ref, sub_ref, pooled_ref, send_ref, place_ref
):
    docs, width = tot_ref.shape
    positions = seg_ref.shape[1]
    member = seg_ref[...] == lax.broadcasted_iota(jnp.int32, (docs, positions), 0)
    counts = jnp.sum(member.astype(jnp.float32), axis=1, keepdims=True)
    mean_rows = tot_ref[...] / counts
    pooled_ref[...] = mean_rows.astype(jnp.bfloat16)
    scale_inv = lax.rsqrt(jnp.sum(mean_rows * mean_rows, axis=1, keepdims=True) + 1e-06)
    unit_rows = (mean_rows * scale_inv).astype(jnp.bfloat16)
    owner = own_ref[...]
    hits = (owner == lax.broadcasted_iota(jnp.int32, (n_owner, docs), 0)).astype(jnp.bfloat16)
    upper = (
        lax.broadcasted_iota(jnp.int32, (docs, docs), 0)
        < lax.broadcasted_iota(jnp.int32, (docs, docs), 1)
    ).astype(jnp.bfloat16)
    before = jnp.dot(hits, upper, preferred_element_type=jnp.float32)
    rank = jnp.sum(before * hits.astype(jnp.float32), axis=0, keepdims=True).astype(jnp.int32)
    place_row = owner * capacity + rank
    place_ref[...] = place_row
    slots = send_ref.shape[0]
    pick = place_row == lax.broadcasted_iota(jnp.int32, (slots, docs), 0)
    send_ref[:, :width] = jnp.dot(
        pick.astype(jnp.bfloat16), unit_rows, preferred_element_type=jnp.float32
    ).astype(jnp.bfloat16)
    key_code = sub_ref[...] + 1
    key_high = jnp.sum(jnp.where(pick, key_code // 64, 0), axis=1, keepdims=True)
    key_low = jnp.sum(jnp.where(pick, key_code % 64, 0), axis=1, keepdims=True)
    lane = lax.broadcasted_iota(jnp.int32, (slots, send_ref.shape[1] - width), 1)
    send_ref[:, width:] = jnp.where(
        lane == 0, key_high, jnp.where(lane == 1, key_low, 0)
    ).astype(jnp.bfloat16)


def epilogue(segments, totals, owner_ids, sub_ids, capacity, n_owner):
    docs, width = totals.shape
    slots = n_owner * capacity
    vmem = pl.BlockSpec(memory_space=pltpu.VMEM)
    return pl.pallas_call(
        functools.partial(epilogue_kernel, capacity, n_owner),
        out_shape=(
            jax.ShapeDtypeStruct((docs, width), jnp.bfloat16),
            jax.ShapeDtypeStruct((slots, width + 128), jnp.bfloat16),
            jax.ShapeDtypeStruct((1, docs), jnp.int32),
        ),
        in_specs=[vmem] * 4,
        out_specs=(vmem, vmem, vmem),
        cost_estimate=pl.CostEstimate(
            flops=2 * slots * docs * (width + 128), transcendentals=docs,
            bytes_accessed=4 * docs * width + 2 * docs * width + 2 * slots * (width + 128),
        ),
    )(segments.reshape(1, -1), totals, owner_ids.reshape(1, docs), sub_ids.reshape(1, docs))


def gather_grp(block):
    n = lax.axis_size("grp")
    chips = n // 2
    core_swap = [(i, i ^ 1) for i in range(n)]
    ring = [
        (i, ((i // 2 + (1 if i % 2 == 0 else chips - 1)) % chips) * 2 + i % 2) for i in range(n)
    ]
    near = lax.ppermute(block, "grp", ring)
    partner = lax.ppermute(block, "grp", core_swap)
    near_partner = lax.ppermute(partner, "grp", ring)
    far = lax.ppermute(near, "grp", ring)
    swapped = [lax.ppermute(piece, "grp", core_swap) for piece in (near, near_partner, far)]
    return [block, partner, near, near_partner, far] + swapped


def per_device(tokens, segment_ids, w_in, b_in, w_out, b_out, owner_ids, sub_ids):
    n_clu = lax.axis_size("clu")
    n_grp = lax.axis_size("grp")
    doc_count = owner_ids.shape[0]
    model_width = tokens.shape[1]
    capacity = 8
    clu_index = lax.axis_index("clu")
    grp_index = lax.axis_index("grp")

    totals = encode(tokens, segment_ids[0], w_in, b_in, w_out, b_out, doc_count)
    pooled, send_rows, place_row = epilogue(
        segment_ids[0], totals, owner_ids, sub_ids, capacity, n_clu
    )
    slot_place = place_row[0]
    row_width = send_rows.shape[1]
    own_rows = lax.all_to_all(
        send_rows.reshape(n_clu, capacity, row_width), "clu", split_axis=0, concat_axis=0,
        tiled=True,
    ).reshape(n_clu * capacity, row_width)
    pieces = gather_grp(own_rows)

    def key_of(rows):
        return (
            rows[:, model_width].astype(jnp.int32) * 64
            + rows[:, model_width + 1].astype(jnp.int32)
            - 1
        )

    own_key = key_of(own_rows)
    own_units = own_rows[:, :model_width]
    slots = n_clu * capacity
    best_sim = jnp.full((slots,), -1.0, jnp.float32)
    for number, piece in enumerate(pieces):
        similar = lax.dot_general(
            own_units, piece[:, :model_width], (((1,), (1,)), ((), ())),
            preferred_element_type=jnp.float32,
        )
        matched = (own_key[:, None] == key_of(piece)[None, :]) & (own_key[:, None] >= 0)
        if number == 0:
            matched = matched & (
                jnp.arange(slots, dtype=jnp.int32)[:, None]
                != jnp.arange(piece.shape[0], dtype=jnp.int32)[None, :]
            )
        best_sim = jnp.maximum(best_sim, jnp.max(jnp.where(matched, similar, -1.0), axis=1))
    lanes = 128
    returned = lax.all_to_all(
        jnp.broadcast_to(best_sim[:, None], (slots, lanes)).reshape(n_clu, capacity, lanes),
        "clu", split_axis=0, concat_axis=0, tiled=True,
    ).reshape(slots, lanes)
    nearest = jnp.sum(
        jnp.where(
            slot_place[None, :] == jnp.arange(slots, dtype=jnp.int32)[:, None],
            returned[:, :1],
            0.0,
        ),
        axis=0,
    )
    return (pooled, nearest)


def solution(mesh):
    in_specs = (
        P(("clu", "grp"), None),
        P(("clu", "grp"), None),
        P(),
        P(),
        P(),
        P(),
        P(("clu", "grp"), None),
        P(("clu", "grp")),
    )
    out_specs = (P(("clu", "grp"), None), P(("clu", "grp")))
    return jax.shard_map(
        per_device, mesh=mesh, in_specs=in_specs, out_specs=out_specs, check_vma=False
    )
```

```python
import functools

import jax
import jax.numpy as jnp
from jax import lax
from jax.experimental import pallas as pl
from jax.experimental.pallas import tpu as pltpu
from jax.sharding import PartitionSpec as P


def encode_kernel(chunk, seg_ref, x_ref, wi_ref, bi_ref, wo_ref, bo_ref, tot_ref):
    step = pl.program_id(0)
    x = x_ref[...]
    ff = wi_ref.shape[1]
    acc = None
    for k in range(ff // chunk):
        part = slice(k * chunk, (k + 1) * chunk)
        pre_act = jnp.dot(x, wi_ref[:, part], preferred_element_type=jnp.float32) + bi_ref[:, part]
        activated = (pre_act * 0.5 * (1.0 + lax.erf(pre_act * 0.7071067811865476))).astype(
            jnp.bfloat16
        )
        term = jnp.dot(activated, wo_ref[part, :], preferred_element_type=jnp.float32)
        acc = term if acc is None else acc + term
    layer_out = (x.astype(jnp.float32) + acc + bo_ref[...]).astype(jnp.bfloat16)
    docs = tot_ref.shape[0]
    member = (
        seg_ref[...] == lax.broadcasted_iota(jnp.int32, (docs, seg_ref.shape[1]), 0)
    ).astype(jnp.bfloat16)
    part_totals = jnp.dot(member, layer_out, preferred_element_type=jnp.float32)

    @pl.when(step == 0)
    def _():
        tot_ref[...] = part_totals

    @pl.when(step != 0)
    def _():
        tot_ref[...] += part_totals


def encode(token_block, segments, w_in, b_in, w_out, b_out, doc_count):
    rows, width = token_block.shape
    ff = w_in.shape[1]
    tile = 512
    flops = 4 * rows * width * ff + 2 * doc_count * rows * width
    totals = pl.pallas_call(
        functools.partial(encode_kernel, 1024),
        out_shape=jax.ShapeDtypeStruct((doc_count, width), jnp.float32),
        grid=(rows // tile,),
        in_specs=[
            pl.BlockSpec((1, tile), lambda i: (0, i)),
            pl.BlockSpec((tile, width), lambda i: (i, 0)),
            pl.BlockSpec((width, ff), lambda i: (0, 0)),
            pl.BlockSpec((1, ff), lambda i: (0, 0)),
            pl.BlockSpec((ff, width), lambda i: (0, 0)),
            pl.BlockSpec((1, width), lambda i: (0, 0)),
        ],
        out_specs=pl.BlockSpec((doc_count, width), lambda i: (0, 0)),
        compiler_params=pltpu.CompilerParams(
            dimension_semantics=("arbitrary",), vmem_limit_bytes=60 * 1024 * 1024
        ),
        cost_estimate=pl.CostEstimate(
            flops=flops, transcendentals=rows * ff, bytes_accessed=2 * rows * width + 8 * width * ff
        ),
    )(segments.reshape(1, rows), token_block, w_in, b_in.reshape(1, ff), w_out, b_out.reshape(1, width))
    return totals


def epilogue_kernel(
    capacity, n_owner, seg_ref, tot_ref, own_ref, sub_ref, pooled_ref, send_ref, place_ref
):
    docs, width = tot_ref.shape
    positions = seg_ref.shape[1]
    member = seg_ref[...] == lax.broadcasted_iota(jnp.int32, (docs, positions), 0)
    counts = jnp.sum(member.astype(jnp.float32), axis=1, keepdims=True)
    mean_rows = tot_ref[...] / counts
    pooled_ref[...] = mean_rows.astype(jnp.bfloat16)
    scale_inv = lax.rsqrt(jnp.sum(mean_rows * mean_rows, axis=1, keepdims=True) + 1e-06)
    unit_rows = (mean_rows * scale_inv).astype(jnp.bfloat16)
    owner = own_ref[...]
    hits = (owner == lax.broadcasted_iota(jnp.int32, (n_owner, docs), 0)).astype(jnp.bfloat16)
    upper = (
        lax.broadcasted_iota(jnp.int32, (docs, docs), 0)
        < lax.broadcasted_iota(jnp.int32, (docs, docs), 1)
    ).astype(jnp.bfloat16)
    before = jnp.dot(hits, upper, preferred_element_type=jnp.float32)
    rank = jnp.sum(before * hits.astype(jnp.float32), axis=0, keepdims=True).astype(jnp.int32)
    place_row = owner * capacity + rank
    place_ref[...] = place_row
    slots = send_ref.shape[0]
    pick = place_row == lax.broadcasted_iota(jnp.int32, (slots, docs), 0)
    send_ref[:, :width] = jnp.dot(
        pick.astype(jnp.bfloat16), unit_rows, preferred_element_type=jnp.float32
    ).astype(jnp.bfloat16)
    key_code = sub_ref[...] + 1
    key_high = jnp.sum(jnp.where(pick, key_code // 64, 0), axis=1, keepdims=True)
    key_low = jnp.sum(jnp.where(pick, key_code % 64, 0), axis=1, keepdims=True)
    lane = lax.broadcasted_iota(jnp.int32, (slots, send_ref.shape[1] - width), 1)
    send_ref[:, width:] = jnp.where(
        lane == 0, key_high, jnp.where(lane == 1, key_low, 0)
    ).astype(jnp.bfloat16)


def epilogue(segments, totals, owner_ids, sub_ids, capacity, n_owner):
    docs, width = totals.shape
    slots = n_owner * capacity
    vmem = pl.BlockSpec(memory_space=pltpu.VMEM)
    return pl.pallas_call(
        functools.partial(epilogue_kernel, capacity, n_owner),
        out_shape=(
            jax.ShapeDtypeStruct((docs, width), jnp.bfloat16),
            jax.ShapeDtypeStruct((slots, width + 128), jnp.bfloat16),
            jax.ShapeDtypeStruct((1, docs), jnp.int32),
        ),
        in_specs=[vmem] * 4,
        out_specs=(vmem, vmem, vmem),
        cost_estimate=pl.CostEstimate(
            flops=2 * slots * docs * (width + 128), transcendentals=docs,
            bytes_accessed=4 * docs * width + 2 * docs * width + 2 * slots * (width + 128),
        ),
    )(segments.reshape(1, -1), totals, owner_ids.reshape(1, docs), sub_ids.reshape(1, docs))


def gather_grp(block):
    n = lax.axis_size("grp")
    chips = n // 2
    core_swap = [(i, i ^ 1) for i in range(n)]
    ring = [
        (i, ((i // 2 + (1 if i % 2 == 0 else chips - 1)) % chips) * 2 + i % 2) for i in range(n)
    ]
    near = lax.ppermute(block, "grp", ring)
    partner = lax.ppermute(block, "grp", core_swap)
    near_partner = lax.ppermute(partner, "grp", ring)
    far = lax.ppermute(near, "grp", ring)
    swapped = [lax.ppermute(piece, "grp", core_swap) for piece in (near, near_partner, far)]
    return [block, partner, near, near_partner, far] + swapped


def per_device(tokens, segment_ids, w_in, b_in, w_out, b_out, owner_ids, sub_ids):
    n_clu = lax.axis_size("clu")
    n_grp = lax.axis_size("grp")
    doc_count = owner_ids.shape[0]
    model_width = tokens.shape[1]
    capacity = 8
    clu_index = lax.axis_index("clu")
    grp_index = lax.axis_index("grp")

    totals = encode(tokens, segment_ids[0], w_in, b_in, w_out, b_out, doc_count)
    pooled, send_rows, place_row = epilogue(
        segment_ids[0], totals, owner_ids, sub_ids, capacity, n_clu
    )
    slot_place = place_row[0]
    row_width = send_rows.shape[1]
    own_rows = lax.all_to_all(
        send_rows.reshape(n_clu, capacity, row_width), "clu", split_axis=0, concat_axis=0,
        tiled=True,
    ).reshape(n_clu * capacity, row_width)
    slots = n_clu * capacity
    own_key = (
        own_rows[:, model_width].astype(jnp.int32) * 64
        + own_rows[:, model_width + 1].astype(jnp.int32)
        - 1
    )
    own_units = own_rows[:, :model_width]
    key_rows = jnp.zeros((8, model_width), jnp.bfloat16)
    key_rows = key_rows.at[0, :slots].set(own_rows[:, model_width])
    key_rows = key_rows.at[1, :slots].set(own_rows[:, model_width + 1])
    pieces = gather_grp(jnp.concatenate([own_units, key_rows], axis=0))

    best_sim = jnp.full((slots,), -1.0, jnp.float32)
    for number, piece in enumerate(pieces):
        similar = lax.dot_general(
            own_units, piece[:slots], (((1,), (1,)), ((), ())),
            preferred_element_type=jnp.float32,
        )
        piece_key = (
            piece[slots, :slots].astype(jnp.int32) * 64
            + piece[slots + 1, :slots].astype(jnp.int32)
            - 1
        )
        matched = (own_key[:, None] == piece_key[None, :]) & (own_key[:, None] >= 0)
        if number == 0:
            matched = matched & (
                jnp.arange(slots, dtype=jnp.int32)[:, None]
                != jnp.arange(slots, dtype=jnp.int32)[None, :]
            )
        best_sim = jnp.maximum(best_sim, jnp.max(jnp.where(matched, similar, -1.0), axis=1))
    lanes = 128
    returned = lax.all_to_all(
        jnp.broadcast_to(best_sim[:, None], (slots, lanes)).reshape(n_clu, capacity, lanes),
        "clu", split_axis=0, concat_axis=0, tiled=True,
    ).reshape(slots, lanes)
    nearest = jnp.sum(
        jnp.where(
            slot_place[None, :] == jnp.arange(slots, dtype=jnp.int32)[:, None],
            returned[:, :1],
            0.0,
        ),
        axis=0,
    )
    return (pooled, nearest)


def solution(mesh):
    in_specs = (
        P(("clu", "grp"), None),
        P(("clu", "grp"), None),
        P(),
        P(),
        P(),
        P(),
        P(("clu", "grp"), None),
        P(("clu", "grp")),
    )
    out_specs = (P(("clu", "grp"), None), P(("clu", "grp")))
    return jax.shard_map(
        per_device, mesh=mesh, in_specs=in_specs, out_specs=out_specs, check_vma=False
    )
```

```python
import functools

import jax
import jax.numpy as jnp
from jax import lax
from jax.experimental import pallas as pl
from jax.experimental.pallas import tpu as pltpu
from jax.sharding import PartitionSpec as P


def encode_kernel(chunk, seg_ref, x_ref, wi_ref, bi_ref, wo_ref, bo_ref, tot_ref):
    step = pl.program_id(0)
    x = x_ref[...]
    ff = wi_ref.shape[1]
    acc = None
    for k in range(ff // chunk):
        part = slice(k * chunk, (k + 1) * chunk)
        pre_act = jnp.dot(x, wi_ref[:, part], preferred_element_type=jnp.float32) + bi_ref[:, part]
        activated = (pre_act * 0.5 * (1.0 + lax.erf(pre_act * 0.7071067811865476))).astype(
            jnp.bfloat16
        )
        term = jnp.dot(activated, wo_ref[part, :], preferred_element_type=jnp.float32)
        acc = term if acc is None else acc + term
    layer_out = (x.astype(jnp.float32) + acc + bo_ref[...]).astype(jnp.bfloat16)
    docs = tot_ref.shape[0]
    member = (
        seg_ref[...] == lax.broadcasted_iota(jnp.int32, (docs, seg_ref.shape[1]), 0)
    ).astype(jnp.bfloat16)
    part_totals = jnp.dot(member, layer_out, preferred_element_type=jnp.float32)

    @pl.when(step == 0)
    def _():
        tot_ref[...] = part_totals

    @pl.when(step != 0)
    def _():
        tot_ref[...] += part_totals


def encode(token_block, segments, w_in, b_in, w_out, b_out, doc_count):
    rows, width = token_block.shape
    ff = w_in.shape[1]
    tile = 512
    flops = 4 * rows * width * ff + 2 * doc_count * rows * width
    totals = pl.pallas_call(
        functools.partial(encode_kernel, 1024),
        out_shape=jax.ShapeDtypeStruct((doc_count, width), jnp.float32),
        grid=(rows // tile,),
        in_specs=[
            pl.BlockSpec((1, tile), lambda i: (0, i)),
            pl.BlockSpec((tile, width), lambda i: (i, 0)),
            pl.BlockSpec((width, ff), lambda i: (0, 0)),
            pl.BlockSpec((1, ff), lambda i: (0, 0)),
            pl.BlockSpec((ff, width), lambda i: (0, 0)),
            pl.BlockSpec((1, width), lambda i: (0, 0)),
        ],
        out_specs=pl.BlockSpec((doc_count, width), lambda i: (0, 0)),
        compiler_params=pltpu.CompilerParams(
            dimension_semantics=("arbitrary",), vmem_limit_bytes=60 * 1024 * 1024
        ),
        cost_estimate=pl.CostEstimate(
            flops=flops, transcendentals=rows * ff, bytes_accessed=2 * rows * width + 8 * width * ff
        ),
    )(segments.reshape(1, rows), token_block, w_in, b_in.reshape(1, ff), w_out, b_out.reshape(1, width))
    return totals


def epilogue_kernel(
    capacity, n_owner, seg_ref, tot_ref, own_ref, sub_ref, pooled_ref, send_ref, place_ref
):
    docs, width = tot_ref.shape
    positions = seg_ref.shape[1]
    member = seg_ref[...] == lax.broadcasted_iota(jnp.int32, (docs, positions), 0)
    counts = jnp.sum(member.astype(jnp.float32), axis=1, keepdims=True)
    mean_rows = tot_ref[...] / counts
    pooled_ref[...] = mean_rows.astype(jnp.bfloat16)
    scale_inv = lax.rsqrt(jnp.sum(mean_rows * mean_rows, axis=1, keepdims=True) + 1e-06)
    unit_rows = (mean_rows * scale_inv).astype(jnp.bfloat16)
    owner = own_ref[...]
    hits = (owner == lax.broadcasted_iota(jnp.int32, (n_owner, docs), 0)).astype(jnp.bfloat16)
    upper = (
        lax.broadcasted_iota(jnp.int32, (docs, docs), 0)
        < lax.broadcasted_iota(jnp.int32, (docs, docs), 1)
    ).astype(jnp.bfloat16)
    before = jnp.dot(hits, upper, preferred_element_type=jnp.float32)
    rank = jnp.sum(before * hits.astype(jnp.float32), axis=0, keepdims=True).astype(jnp.int32)
    place_row = owner * capacity + rank
    place_ref[...] = place_row
    slots = send_ref.shape[0]
    pick = place_row == lax.broadcasted_iota(jnp.int32, (slots, docs), 0)
    send_ref[:, :width] = jnp.dot(
        pick.astype(jnp.bfloat16), unit_rows, preferred_element_type=jnp.float32
    ).astype(jnp.bfloat16)
    key_code = sub_ref[...] + 1
    key_high = jnp.sum(jnp.where(pick, key_code // 64, 0), axis=1, keepdims=True)
    key_low = jnp.sum(jnp.where(pick, key_code % 64, 0), axis=1, keepdims=True)
    lane = lax.broadcasted_iota(jnp.int32, (slots, send_ref.shape[1] - width), 1)
    send_ref[:, width:] = jnp.where(
        lane == 0, key_high, jnp.where(lane == 1, key_low, 0)
    ).astype(jnp.bfloat16)


def epilogue(segments, totals, owner_ids, sub_ids, capacity, n_owner):
    docs, width = totals.shape
    slots = n_owner * capacity
    vmem = pl.BlockSpec(memory_space=pltpu.VMEM)
    return pl.pallas_call(
        functools.partial(epilogue_kernel, capacity, n_owner),
        out_shape=(
            jax.ShapeDtypeStruct((docs, width), jnp.bfloat16),
            jax.ShapeDtypeStruct((slots, width + 128), jnp.bfloat16),
            jax.ShapeDtypeStruct((1, docs), jnp.int32),
        ),
        in_specs=[vmem] * 4,
        out_specs=(vmem, vmem, vmem),
        cost_estimate=pl.CostEstimate(
            flops=2 * slots * docs * (width + 128), transcendentals=docs,
            bytes_accessed=4 * docs * width + 2 * docs * width + 2 * slots * (width + 128),
        ),
    )(segments.reshape(1, -1), totals, owner_ids.reshape(1, docs), sub_ids.reshape(1, docs))


def gather_grp(block):
    n = lax.axis_size("grp")
    chips = n // 2
    core_swap = [(i, i ^ 1) for i in range(n)]
    ring = [
        (i, ((i // 2 + (1 if i % 2 == 0 else chips - 1)) % chips) * 2 + i % 2) for i in range(n)
    ]
    cross = [
        (i, ((i // 2 + (chips - 1 if i % 2 == 0 else 1)) % chips) * 2 + (1 - i % 2))
        for i in range(n)
    ]
    near = lax.ppermute(block, "grp", ring)
    near_partner = lax.ppermute(block, "grp", cross)
    partner = lax.ppermute(block, "grp", core_swap)
    far = lax.ppermute(near, "grp", ring)
    swapped = [lax.ppermute(piece, "grp", core_swap) for piece in (near, near_partner, far)]
    return [block, partner, near, near_partner, far] + swapped


def per_device(tokens, segment_ids, w_in, b_in, w_out, b_out, owner_ids, sub_ids):
    n_clu = lax.axis_size("clu")
    n_grp = lax.axis_size("grp")
    doc_count = owner_ids.shape[0]
    model_width = tokens.shape[1]
    capacity = 8
    clu_index = lax.axis_index("clu")
    grp_index = lax.axis_index("grp")

    totals = encode(tokens, segment_ids[0], w_in, b_in, w_out, b_out, doc_count)
    pooled, send_rows, place_row = epilogue(
        segment_ids[0], totals, owner_ids, sub_ids, capacity, n_clu
    )
    slot_place = place_row[0]
    row_width = send_rows.shape[1]
    own_rows = lax.all_to_all(
        send_rows.reshape(n_clu, capacity, row_width), "clu", split_axis=0, concat_axis=0,
        tiled=True,
    ).reshape(n_clu * capacity, row_width)
    slots = n_clu * capacity
    own_key = (
        own_rows[:, model_width].astype(jnp.int32) * 64
        + own_rows[:, model_width + 1].astype(jnp.int32)
        - 1
    )
    own_units = own_rows[:, :model_width]
    key_rows = jnp.zeros((8, model_width), jnp.bfloat16)
    key_rows = key_rows.at[0, :slots].set(own_rows[:, model_width])
    key_rows = key_rows.at[1, :slots].set(own_rows[:, model_width + 1])
    pieces = gather_grp(jnp.concatenate([own_units, key_rows], axis=0))

    best_sim = jnp.full((slots,), -1.0, jnp.float32)
    for number, piece in enumerate(pieces):
        similar = lax.dot_general(
            own_units, piece[:slots], (((1,), (1,)), ((), ())),
            preferred_element_type=jnp.float32,
        )
        piece_key = (
            piece[slots, :slots].astype(jnp.int32) * 64
            + piece[slots + 1, :slots].astype(jnp.int32)
            - 1
        )
        matched = (own_key[:, None] == piece_key[None, :]) & (own_key[:, None] >= 0)
        if number == 0:
            matched = matched & (
                jnp.arange(slots, dtype=jnp.int32)[:, None]
                != jnp.arange(slots, dtype=jnp.int32)[None, :]
            )
        best_sim = jnp.maximum(best_sim, jnp.max(jnp.where(matched, similar, -1.0), axis=1))
    lanes = 128
    returned = lax.all_to_all(
        jnp.broadcast_to(best_sim[:, None], (slots, lanes)).reshape(n_clu, capacity, lanes),
        "clu", split_axis=0, concat_axis=0, tiled=True,
    ).reshape(slots, lanes)
    nearest = jnp.sum(
        jnp.where(
            slot_place[None, :] == jnp.arange(slots, dtype=jnp.int32)[:, None],
            returned[:, :1],
            0.0,
        ),
        axis=0,
    )
    return (pooled, nearest)


def solution(mesh):
    in_specs = (
        P(("clu", "grp"), None),
        P(("clu", "grp"), None),
        P(),
        P(),
        P(),
        P(),
        P(("clu", "grp"), None),
        P(("clu", "grp")),
    )
    out_specs = (P(("clu", "grp"), None), P(("clu", "grp")))
    return jax.shard_map(
        per_device, mesh=mesh, in_specs=in_specs, out_specs=out_specs, check_vma=False
    )
```

```python
import functools

import jax
import jax.numpy as jnp
from jax import lax
from jax.experimental import pallas as pl
from jax.experimental.pallas import tpu as pltpu
from jax.sharding import PartitionSpec as P


def encode_kernel(chunk, seg_ref, x_ref, wi_ref, bi_ref, wo_ref, bo_ref, tot_ref):
    step = pl.program_id(0)
    x = x_ref[...]
    ff = wi_ref.shape[1]
    acc = None
    for k in range(ff // chunk):
        part = slice(k * chunk, (k + 1) * chunk)
        pre_act = jnp.dot(x, wi_ref[:, part], preferred_element_type=jnp.float32) + bi_ref[:, part]
        activated = (pre_act * 0.5 * (1.0 + lax.erf(pre_act * 0.7071067811865476))).astype(
            jnp.bfloat16
        )
        term = jnp.dot(activated, wo_ref[part, :], preferred_element_type=jnp.float32)
        acc = term if acc is None else acc + term
    layer_out = (x.astype(jnp.float32) + acc + bo_ref[...]).astype(jnp.bfloat16)
    docs = tot_ref.shape[0]
    member = (
        seg_ref[...] == lax.broadcasted_iota(jnp.int32, (docs, seg_ref.shape[1]), 0)
    ).astype(jnp.bfloat16)
    part_totals = jnp.dot(member, layer_out, preferred_element_type=jnp.float32)

    @pl.when(step == 0)
    def _():
        tot_ref[...] = part_totals

    @pl.when(step != 0)
    def _():
        tot_ref[...] += part_totals


def encode(token_block, segments, w_in, b_in, w_out, b_out, doc_count):
    rows, width = token_block.shape
    ff = w_in.shape[1]
    tile = 512
    flops = 4 * rows * width * ff + 2 * doc_count * rows * width
    totals = pl.pallas_call(
        functools.partial(encode_kernel, 1024),
        out_shape=jax.ShapeDtypeStruct((doc_count, width), jnp.float32),
        grid=(rows // tile,),
        in_specs=[
            pl.BlockSpec((1, tile), lambda i: (0, i)),
            pl.BlockSpec((tile, width), lambda i: (i, 0)),
            pl.BlockSpec((width, ff), lambda i: (0, 0)),
            pl.BlockSpec((1, ff), lambda i: (0, 0)),
            pl.BlockSpec((ff, width), lambda i: (0, 0)),
            pl.BlockSpec((1, width), lambda i: (0, 0)),
        ],
        out_specs=pl.BlockSpec((doc_count, width), lambda i: (0, 0)),
        compiler_params=pltpu.CompilerParams(
            dimension_semantics=("arbitrary",), vmem_limit_bytes=60 * 1024 * 1024
        ),
        cost_estimate=pl.CostEstimate(
            flops=flops, transcendentals=rows * ff, bytes_accessed=2 * rows * width + 8 * width * ff
        ),
    )(segments.reshape(1, rows), token_block, w_in, b_in.reshape(1, ff), w_out, b_out.reshape(1, width))
    return totals


def epilogue_kernel(
    capacity, n_owner, seg_ref, tot_ref, own_ref, sub_ref, pooled_ref, send_ref, place_ref
):
    docs, width = tot_ref.shape
    positions = seg_ref.shape[1]
    member = seg_ref[...] == lax.broadcasted_iota(jnp.int32, (docs, positions), 0)
    counts = jnp.sum(member.astype(jnp.float32), axis=1, keepdims=True)
    mean_rows = tot_ref[...] / counts
    pooled_ref[...] = mean_rows.astype(jnp.bfloat16)
    scale_inv = lax.rsqrt(jnp.sum(mean_rows * mean_rows, axis=1, keepdims=True) + 1e-06)
    unit_rows = (mean_rows * scale_inv).astype(jnp.bfloat16)
    owner = own_ref[...]
    hits = (owner == lax.broadcasted_iota(jnp.int32, (n_owner, docs), 0)).astype(jnp.bfloat16)
    upper = (
        lax.broadcasted_iota(jnp.int32, (docs, docs), 0)
        < lax.broadcasted_iota(jnp.int32, (docs, docs), 1)
    ).astype(jnp.bfloat16)
    before = jnp.dot(hits, upper, preferred_element_type=jnp.float32)
    rank = jnp.sum(before * hits.astype(jnp.float32), axis=0, keepdims=True).astype(jnp.int32)
    place_row = owner * capacity + rank
    place_ref[...] = place_row
    slots = send_ref.shape[0]
    pick = place_row == lax.broadcasted_iota(jnp.int32, (slots, docs), 0)
    send_ref[:, :width] = jnp.dot(
        pick.astype(jnp.bfloat16), unit_rows, preferred_element_type=jnp.float32
    ).astype(jnp.bfloat16)
    key_code = sub_ref[...] + 1
    key_high = jnp.sum(jnp.where(pick, key_code // 64, 0), axis=1, keepdims=True)
    key_low = jnp.sum(jnp.where(pick, key_code % 64, 0), axis=1, keepdims=True)
    lane = lax.broadcasted_iota(jnp.int32, (slots, send_ref.shape[1] - width), 1)
    send_ref[:, width:] = jnp.where(
        lane == 0, key_high, jnp.where(lane == 1, key_low, 0)
    ).astype(jnp.bfloat16)


def epilogue(segments, totals, owner_ids, sub_ids, capacity, n_owner):
    docs, width = totals.shape
    slots = n_owner * capacity
    vmem = pl.BlockSpec(memory_space=pltpu.VMEM)
    return pl.pallas_call(
        functools.partial(epilogue_kernel, capacity, n_owner),
        out_shape=(
            jax.ShapeDtypeStruct((docs, width), jnp.bfloat16),
            jax.ShapeDtypeStruct((slots, width + 128), jnp.bfloat16),
            jax.ShapeDtypeStruct((1, docs), jnp.int32),
        ),
        in_specs=[vmem] * 4,
        out_specs=(vmem, vmem, vmem),
        cost_estimate=pl.CostEstimate(
            flops=2 * slots * docs * (width + 128), transcendentals=docs,
            bytes_accessed=4 * docs * width + 2 * docs * width + 2 * slots * (width + 128),
        ),
    )(segments.reshape(1, -1), totals, owner_ids.reshape(1, docs), sub_ids.reshape(1, docs))


def gather_grp(block):
    n = lax.axis_size("grp")
    chips = n // 2
    core_swap = [(i, i ^ 1) for i in range(n)]
    ring = [
        (i, ((i // 2 + (1 if i % 2 == 0 else chips - 1)) % chips) * 2 + i % 2) for i in range(n)
    ]
    cross = [
        (i, ((i // 2 + (chips - 1 if i % 2 == 0 else 1)) % chips) * 2 + (1 - i % 2))
        for i in range(n)
    ]
    near = lax.ppermute(block, "grp", ring)
    partner = lax.ppermute(block, "grp", core_swap)
    held, near = lax.optimization_barrier((block, near))
    near_partner = lax.ppermute(held, "grp", cross)
    far = lax.ppermute(near, "grp", ring)
    swapped = [lax.ppermute(piece, "grp", core_swap) for piece in (near, near_partner, far)]
    return [block, partner, near, near_partner, far] + swapped


def per_device(tokens, segment_ids, w_in, b_in, w_out, b_out, owner_ids, sub_ids):
    n_clu = lax.axis_size("clu")
    n_grp = lax.axis_size("grp")
    doc_count = owner_ids.shape[0]
    model_width = tokens.shape[1]
    capacity = 8
    clu_index = lax.axis_index("clu")
    grp_index = lax.axis_index("grp")

    totals = encode(tokens, segment_ids[0], w_in, b_in, w_out, b_out, doc_count)
    pooled, send_rows, place_row = epilogue(
        segment_ids[0], totals, owner_ids, sub_ids, capacity, n_clu
    )
    slot_place = place_row[0]
    row_width = send_rows.shape[1]
    own_rows = lax.all_to_all(
        send_rows.reshape(n_clu, capacity, row_width), "clu", split_axis=0, concat_axis=0,
        tiled=True,
    ).reshape(n_clu * capacity, row_width)
    slots = n_clu * capacity
    own_key = (
        own_rows[:, model_width].astype(jnp.int32) * 64
        + own_rows[:, model_width + 1].astype(jnp.int32)
        - 1
    )
    own_units = own_rows[:, :model_width]
    key_rows = jnp.zeros((8, model_width), jnp.bfloat16)
    key_rows = key_rows.at[0, :slots].set(own_rows[:, model_width])
    key_rows = key_rows.at[1, :slots].set(own_rows[:, model_width + 1])
    pieces = gather_grp(jnp.concatenate([own_units, key_rows], axis=0))

    best_sim = jnp.full((slots,), -1.0, jnp.float32)
    for number, piece in enumerate(pieces):
        similar = lax.dot_general(
            own_units, piece[:slots], (((1,), (1,)), ((), ())),
            preferred_element_type=jnp.float32,
        )
        piece_key = (
            piece[slots, :slots].astype(jnp.int32) * 64
            + piece[slots + 1, :slots].astype(jnp.int32)
            - 1
        )
        matched = (own_key[:, None] == piece_key[None, :]) & (own_key[:, None] >= 0)
        if number == 0:
            matched = matched & (
                jnp.arange(slots, dtype=jnp.int32)[:, None]
                != jnp.arange(slots, dtype=jnp.int32)[None, :]
            )
        best_sim = jnp.maximum(best_sim, jnp.max(jnp.where(matched, similar, -1.0), axis=1))
    lanes = 128
    returned = lax.all_to_all(
        jnp.broadcast_to(best_sim[:, None], (slots, lanes)).reshape(n_clu, capacity, lanes),
        "clu", split_axis=0, concat_axis=0, tiled=True,
    ).reshape(slots, lanes)
    nearest = jnp.sum(
        jnp.where(
            slot_place[None, :] == jnp.arange(slots, dtype=jnp.int32)[:, None],
            returned[:, :1],
            0.0,
        ),
        axis=0,
    )
    return (pooled, nearest)


def solution(mesh):
    in_specs = (
        P(("clu", "grp"), None),
        P(("clu", "grp"), None),
        P(),
        P(),
        P(),
        P(),
        P(("clu", "grp"), None),
        P(("clu", "grp")),
    )
    out_specs = (P(("clu", "grp"), None), P(("clu", "grp")))
    return jax.shard_map(
        per_device, mesh=mesh, in_specs=in_specs, out_specs=out_specs, check_vma=False
    )
```

```python
import functools

import jax
import jax.numpy as jnp
from jax import lax
from jax.experimental import pallas as pl
from jax.experimental.pallas import tpu as pltpu
from jax.sharding import PartitionSpec as P


def encode_kernel(
    chunk, capacity, n_owner, seg_ref, x_ref, wi_ref, bi_ref, wo_ref, bo_ref, seg_all_ref,
    own_ref, sub_ref, pooled_ref, send_ref, place_ref, tot_ref,
):
    step = pl.program_id(0)
    x = x_ref[...]
    ff = wi_ref.shape[1]
    acc = None
    for k in range(ff // chunk):
        part = slice(k * chunk, (k + 1) * chunk)
        pre_act = jnp.dot(x, wi_ref[:, part], preferred_element_type=jnp.float32) + bi_ref[:, part]
        activated = (pre_act * 0.5 * (1.0 + lax.erf(pre_act * 0.7071067811865476))).astype(
            jnp.bfloat16
        )
        term = jnp.dot(activated, wo_ref[part, :], preferred_element_type=jnp.float32)
        acc = term if acc is None else acc + term
    layer_out = (x.astype(jnp.float32) + acc + bo_ref[...]).astype(jnp.bfloat16)
    docs = tot_ref.shape[0]
    member = (
        seg_ref[...] == lax.broadcasted_iota(jnp.int32, (docs, seg_ref.shape[1]), 0)
    ).astype(jnp.bfloat16)
    part_totals = jnp.dot(member, layer_out, preferred_element_type=jnp.float32)

    @pl.when(step == 0)
    def _():
        tot_ref[...] = part_totals

    @pl.when(step != 0)
    def _():
        tot_ref[...] += part_totals

    @pl.when(step == pl.num_programs(0) - 1)
    def _():
        finish(capacity, n_owner, seg_all_ref, tot_ref, own_ref, sub_ref, pooled_ref, send_ref,
               place_ref)


def finish(capacity, n_owner, seg_ref, tot_ref, own_ref, sub_ref, pooled_ref, send_ref, place_ref):
    docs, width = tot_ref.shape
    positions = seg_ref.shape[1]
    member = seg_ref[...] == lax.broadcasted_iota(jnp.int32, (docs, positions), 0)
    counts = jnp.sum(member.astype(jnp.float32), axis=1, keepdims=True)
    mean_rows = tot_ref[...] / counts
    pooled_ref[...] = mean_rows.astype(jnp.bfloat16)
    scale_inv = lax.rsqrt(jnp.sum(mean_rows * mean_rows, axis=1, keepdims=True) + 1e-06)
    unit_rows = (mean_rows * scale_inv).astype(jnp.bfloat16)
    owner = own_ref[...]
    hits = (owner == lax.broadcasted_iota(jnp.int32, (n_owner, docs), 0)).astype(jnp.bfloat16)
    upper = (
        lax.broadcasted_iota(jnp.int32, (docs, docs), 0)
        < lax.broadcasted_iota(jnp.int32, (docs, docs), 1)
    ).astype(jnp.bfloat16)
    before = jnp.dot(hits, upper, preferred_element_type=jnp.float32)
    rank = jnp.sum(before * hits.astype(jnp.float32), axis=0, keepdims=True).astype(jnp.int32)
    place_row = owner * capacity + rank
    place_ref[...] = place_row
    slots = send_ref.shape[0]
    pick = place_row == lax.broadcasted_iota(jnp.int32, (slots, docs), 0)
    send_ref[:, :width] = jnp.dot(
        pick.astype(jnp.bfloat16), unit_rows, preferred_element_type=jnp.float32
    ).astype(jnp.bfloat16)
    key_code = sub_ref[...] + 1
    key_high = jnp.sum(jnp.where(pick, key_code // 64, 0), axis=1, keepdims=True)
    key_low = jnp.sum(jnp.where(pick, key_code % 64, 0), axis=1, keepdims=True)
    lane = lax.broadcasted_iota(jnp.int32, (slots, send_ref.shape[1] - width), 1)
    send_ref[:, width:] = jnp.where(
        lane == 0, key_high, jnp.where(lane == 1, key_low, 0)
    ).astype(jnp.bfloat16)


def encode(token_block, segments, w_in, b_in, w_out, b_out, owner_ids, sub_ids, capacity, n_owner):
    rows, width = token_block.shape
    ff = w_in.shape[1]
    docs = owner_ids.shape[0]
    slots = n_owner * capacity
    tile = 512
    flops = 4 * rows * width * ff + 2 * docs * rows * width + 2 * slots * docs * width
    whole = lambda i: (0, 0)
    return pl.pallas_call(
        functools.partial(encode_kernel, 1024, capacity, n_owner),
        out_shape=(
            jax.ShapeDtypeStruct((docs, width), jnp.bfloat16),
            jax.ShapeDtypeStruct((slots, width + 128), jnp.bfloat16),
            jax.ShapeDtypeStruct((1, docs), jnp.int32),
        ),
        grid=(rows // tile,),
        in_specs=[
            pl.BlockSpec((1, tile), lambda i: (0, i)),
            pl.BlockSpec((tile, width), lambda i: (i, 0)),
            pl.BlockSpec((width, ff), whole),
            pl.BlockSpec((1, ff), whole),
            pl.BlockSpec((ff, width), whole),
            pl.BlockSpec((1, width), whole),
            pl.BlockSpec((1, rows), whole),
            pl.BlockSpec((1, docs), whole),
            pl.BlockSpec((1, docs), whole),
        ],
        out_specs=(
            pl.BlockSpec((docs, width), whole),
            pl.BlockSpec((slots, width + 128), whole),
            pl.BlockSpec((1, docs), whole),
        ),
        scratch_shapes=[pltpu.VMEM((docs, width), jnp.float32)],
        compiler_params=pltpu.CompilerParams(
            dimension_semantics=("arbitrary",), vmem_limit_bytes=60 * 1024 * 1024
        ),
        cost_estimate=pl.CostEstimate(
            flops=flops, transcendentals=rows * ff,
            bytes_accessed=2 * rows * width + 8 * width * ff + 2 * slots * (width + 128),
        ),
    )(
        segments.reshape(1, rows), token_block, w_in, b_in.reshape(1, ff), w_out,
        b_out.reshape(1, width), segments.reshape(1, rows), owner_ids.reshape(1, docs),
        sub_ids.reshape(1, docs),
    )


def gather_grp(block):
    n = lax.axis_size("grp")
    chips = n // 2
    core_swap = [(i, i ^ 1) for i in range(n)]
    ring = [
        (i, ((i // 2 + (1 if i % 2 == 0 else chips - 1)) % chips) * 2 + i % 2) for i in range(n)
    ]
    near = lax.ppermute(block, "grp", ring)
    partner = lax.ppermute(block, "grp", core_swap)
    near_partner = lax.ppermute(partner, "grp", ring)
    far = lax.ppermute(near, "grp", ring)
    swapped = [lax.ppermute(piece, "grp", core_swap) for piece in (near, near_partner, far)]
    return [block, partner, near, near_partner, far] + swapped


def per_device(tokens, segment_ids, w_in, b_in, w_out, b_out, owner_ids, sub_ids):
    n_clu = lax.axis_size("clu")
    n_grp = lax.axis_size("grp")
    doc_count = owner_ids.shape[0]
    model_width = tokens.shape[1]
    capacity = 8
    clu_index = lax.axis_index("clu")
    grp_index = lax.axis_index("grp")

    pooled, send_rows, place_row = encode(
        tokens, segment_ids[0], w_in, b_in, w_out, b_out, owner_ids, sub_ids, capacity, n_clu
    )
    slot_place = place_row[0]
    row_width = send_rows.shape[1]
    own_rows = lax.all_to_all(
        send_rows.reshape(n_clu, capacity, row_width), "clu", split_axis=0, concat_axis=0,
        tiled=True,
    ).reshape(n_clu * capacity, row_width)
    pieces = gather_grp(own_rows)

    def key_of(rows):
        return (
            rows[:, model_width].astype(jnp.int32) * 64
            + rows[:, model_width + 1].astype(jnp.int32)
            - 1
        )

    own_key = key_of(own_rows)
    own_units = own_rows[:, :model_width]
    slots = n_clu * capacity
    best_sim = jnp.full((slots,), -1.0, jnp.float32)
    for number, piece in enumerate(pieces):
        similar = lax.dot_general(
            own_units, piece[:, :model_width], (((1,), (1,)), ((), ())),
            preferred_element_type=jnp.float32,
        )
        matched = (own_key[:, None] == key_of(piece)[None, :]) & (own_key[:, None] >= 0)
        if number == 0:
            matched = matched & (
                jnp.arange(slots, dtype=jnp.int32)[:, None]
                != jnp.arange(piece.shape[0], dtype=jnp.int32)[None, :]
            )
        best_sim = jnp.maximum(best_sim, jnp.max(jnp.where(matched, similar, -1.0), axis=1))
    lanes = 128
    returned = lax.all_to_all(
        jnp.broadcast_to(best_sim[:, None], (slots, lanes)).reshape(n_clu, capacity, lanes),
        "clu", split_axis=0, concat_axis=0, tiled=True,
    ).reshape(slots, lanes)
    nearest = jnp.sum(
        jnp.where(
            slot_place[None, :] == jnp.arange(slots, dtype=jnp.int32)[:, None],
            returned[:, :1],
            0.0,
        ),
        axis=0,
    )
    return (pooled, nearest)


def solution(mesh):
    in_specs = (
        P(("clu", "grp"), None),
        P(("clu", "grp"), None),
        P(),
        P(),
        P(),
        P(),
        P(("clu", "grp"), None),
        P(("clu", "grp")),
    )
    out_specs = (P(("clu", "grp"), None), P(("clu", "grp")))
    return jax.shard_map(
        per_device, mesh=mesh, in_specs=in_specs, out_specs=out_specs, check_vma=False
    )
```

```python
import functools

import jax
import jax.numpy as jnp
from jax import lax
from jax.experimental import pallas as pl
from jax.experimental.pallas import tpu as pltpu
from jax.sharding import PartitionSpec as P


def encode_kernel(
    chunk, capacity, n_owner, seg_ref, x_ref, wi_ref, bi_ref, wo_ref, bo_ref, seg_all_ref,
    own_ref, sub_ref, pooled_ref, send_ref, place_ref, tot_ref,
):
    step = pl.program_id(0)
    x = x_ref[...]
    ff = wi_ref.shape[1]
    acc = None
    for k in range(ff // chunk):
        part = slice(k * chunk, (k + 1) * chunk)
        pre_act = jnp.dot(x, wi_ref[:, part], preferred_element_type=jnp.float32) + bi_ref[:, part]
        activated = (pre_act * 0.5 * (1.0 + lax.erf(pre_act * 0.7071067811865476))).astype(
            jnp.bfloat16
        )
        term = jnp.dot(activated, wo_ref[part, :], preferred_element_type=jnp.float32)
        acc = term if acc is None else acc + term
    layer_out = (x.astype(jnp.float32) + acc + bo_ref[...]).astype(jnp.bfloat16)
    docs = tot_ref.shape[0]
    member = (
        seg_ref[...] == lax.broadcasted_iota(jnp.int32, (docs, seg_ref.shape[1]), 0)
    ).astype(jnp.bfloat16)
    part_totals = jnp.dot(member, layer_out, preferred_element_type=jnp.float32)

    @pl.when(step == 0)
    def _():
        tot_ref[...] = part_totals

    @pl.when(step != 0)
    def _():
        tot_ref[...] += part_totals

    @pl.when(step == pl.num_programs(0) - 1)
    def _():
        finish(capacity, n_owner, seg_all_ref, tot_ref, own_ref, sub_ref, pooled_ref, send_ref,
               place_ref)


def finish(capacity, n_owner, seg_ref, tot_ref, own_ref, sub_ref, pooled_ref, send_ref, place_ref):
    docs, width = tot_ref.shape
    positions = seg_ref.shape[1]
    member = seg_ref[...] == lax.broadcasted_iota(jnp.int32, (docs, positions), 0)
    counts = jnp.sum(member.astype(jnp.float32), axis=1, keepdims=True)
    mean_rows = tot_ref[...] / counts
    pooled_ref[...] = mean_rows.astype(jnp.bfloat16)
    scale_inv = lax.rsqrt(jnp.sum(mean_rows * mean_rows, axis=1, keepdims=True) + 1e-06)
    unit_rows = (mean_rows * scale_inv).astype(jnp.bfloat16)
    owner = own_ref[...]
    hits = (owner == lax.broadcasted_iota(jnp.int32, (n_owner, docs), 0)).astype(jnp.bfloat16)
    upper = (
        lax.broadcasted_iota(jnp.int32, (docs, docs), 0)
        < lax.broadcasted_iota(jnp.int32, (docs, docs), 1)
    ).astype(jnp.bfloat16)
    before = jnp.dot(hits, upper, preferred_element_type=jnp.float32)
    rank = jnp.sum(before * hits.astype(jnp.float32), axis=0, keepdims=True).astype(jnp.int32)
    place_row = owner * capacity + rank
    place_ref[...] = place_row
    slots = send_ref.shape[0]
    pick = place_row == lax.broadcasted_iota(jnp.int32, (slots, docs), 0)
    send_ref[:, :width] = jnp.dot(
        pick.astype(jnp.bfloat16), unit_rows, preferred_element_type=jnp.float32
    ).astype(jnp.bfloat16)
    key_code = sub_ref[...] + 1
    key_high = jnp.sum(jnp.where(pick, key_code // 64, 0), axis=1, keepdims=True)
    key_low = jnp.sum(jnp.where(pick, key_code % 64, 0), axis=1, keepdims=True)
    lane = lax.broadcasted_iota(jnp.int32, (slots, send_ref.shape[1] - width), 1)
    send_ref[:, width:] = jnp.where(
        lane == 0, key_high, jnp.where(lane == 1, key_low, 0)
    ).astype(jnp.bfloat16)


def encode(token_block, segments, w_in, b_in, w_out, b_out, owner_ids, sub_ids, capacity, n_owner):
    rows, width = token_block.shape
    ff = w_in.shape[1]
    docs = owner_ids.shape[0]
    slots = n_owner * capacity
    tile = 512
    flops = 4 * rows * width * ff + 2 * docs * rows * width + 2 * slots * docs * width
    whole = lambda i: (0, 0)
    return pl.pallas_call(
        functools.partial(encode_kernel, 1024, capacity, n_owner),
        out_shape=(
            jax.ShapeDtypeStruct((docs, width), jnp.bfloat16),
            jax.ShapeDtypeStruct((slots, width + 128), jnp.bfloat16),
            jax.ShapeDtypeStruct((1, docs), jnp.int32),
        ),
        grid=(rows // tile,),
        in_specs=[
            pl.BlockSpec((1, tile), lambda i: (0, i)),
            pl.BlockSpec((tile, width), lambda i: (i, 0)),
            pl.BlockSpec((width, ff), whole),
            pl.BlockSpec((1, ff), whole),
            pl.BlockSpec((ff, width), whole),
            pl.BlockSpec((1, width), whole),
            pl.BlockSpec((1, rows), whole),
            pl.BlockSpec((1, docs), whole),
            pl.BlockSpec((1, docs), whole),
        ],
        out_specs=(
            pl.BlockSpec((docs, width), whole),
            pl.BlockSpec((slots, width + 128), whole),
            pl.BlockSpec((1, docs), whole),
        ),
        scratch_shapes=[pltpu.VMEM((docs, width), jnp.float32)],
        compiler_params=pltpu.CompilerParams(
            dimension_semantics=("arbitrary",), vmem_limit_bytes=60 * 1024 * 1024
        ),
        cost_estimate=pl.CostEstimate(
            flops=flops, transcendentals=rows * ff,
            bytes_accessed=2 * rows * width + 8 * width * ff + 2 * slots * (width + 128),
        ),
    )(
        segments.reshape(1, rows), token_block, w_in, b_in.reshape(1, ff), w_out,
        b_out.reshape(1, width), segments.reshape(1, rows), owner_ids.reshape(1, docs),
        sub_ids.reshape(1, docs),
    )


def gather_grp(block):
    n = lax.axis_size("grp")
    chips = n // 2
    core_swap = [(i, i ^ 1) for i in range(n)]
    ring = [
        (i, ((i // 2 + (1 if i % 2 == 0 else chips - 1)) % chips) * 2 + i % 2) for i in range(n)
    ]
    near = lax.ppermute(block, "grp", ring)
    partner = lax.ppermute(block, "grp", core_swap)
    near_partner = lax.ppermute(partner, "grp", ring)
    far = lax.ppermute(near, "grp", ring)
    early = lax.ppermute(jnp.concatenate([near, near_partner], axis=0), "grp", core_swap)
    swapped = [early, lax.ppermute(far, "grp", core_swap)]
    return [block, partner, near, near_partner, far] + swapped


def per_device(tokens, segment_ids, w_in, b_in, w_out, b_out, owner_ids, sub_ids):
    n_clu = lax.axis_size("clu")
    n_grp = lax.axis_size("grp")
    doc_count = owner_ids.shape[0]
    model_width = tokens.shape[1]
    capacity = 8
    clu_index = lax.axis_index("clu")
    grp_index = lax.axis_index("grp")

    pooled, send_rows, place_row = encode(
        tokens, segment_ids[0], w_in, b_in, w_out, b_out, owner_ids, sub_ids, capacity, n_clu
    )
    slot_place = place_row[0]
    row_width = send_rows.shape[1]
    own_rows = lax.all_to_all(
        send_rows.reshape(n_clu, capacity, row_width), "clu", split_axis=0, concat_axis=0,
        tiled=True,
    ).reshape(n_clu * capacity, row_width)
    pieces = gather_grp(own_rows)

    def key_of(rows):
        return (
            rows[:, model_width].astype(jnp.int32) * 64
            + rows[:, model_width + 1].astype(jnp.int32)
            - 1
        )

    own_key = key_of(own_rows)
    own_units = own_rows[:, :model_width]
    slots = n_clu * capacity
    best_sim = jnp.full((slots,), -1.0, jnp.float32)
    for number, piece in enumerate(pieces):
        similar = lax.dot_general(
            own_units, piece[:, :model_width], (((1,), (1,)), ((), ())),
            preferred_element_type=jnp.float32,
        )
        matched = (own_key[:, None] == key_of(piece)[None, :]) & (own_key[:, None] >= 0)
        if number == 0:
            matched = matched & (
                jnp.arange(slots, dtype=jnp.int32)[:, None]
                != jnp.arange(piece.shape[0], dtype=jnp.int32)[None, :]
            )
        best_sim = jnp.maximum(best_sim, jnp.max(jnp.where(matched, similar, -1.0), axis=1))
    lanes = 128
    returned = lax.all_to_all(
        jnp.broadcast_to(best_sim[:, None], (slots, lanes)).reshape(n_clu, capacity, lanes),
        "clu", split_axis=0, concat_axis=0, tiled=True,
    ).reshape(slots, lanes)
    nearest = jnp.sum(
        jnp.where(
            slot_place[None, :] == jnp.arange(slots, dtype=jnp.int32)[:, None],
            returned[:, :1],
            0.0,
        ),
        axis=0,
    )
    return (pooled, nearest)


def solution(mesh):
    in_specs = (
        P(("clu", "grp"), None),
        P(("clu", "grp"), None),
        P(),
        P(),
        P(),
        P(),
        P(("clu", "grp"), None),
        P(("clu", "grp")),
    )
    out_specs = (P(("clu", "grp"), None), P(("clu", "grp")))
    return jax.shard_map(
        per_device, mesh=mesh, in_specs=in_specs, out_specs=out_specs, check_vma=False
    )
```

```python
import functools

import jax
import jax.numpy as jnp
from jax import lax
from jax.experimental import pallas as pl
from jax.experimental.pallas import tpu as pltpu
from jax.sharding import PartitionSpec as P


def encode_kernel(
    chunk, capacity, n_owner, seg_ref, x_ref, wi_ref, bi_ref, wo_ref, bo_ref, seg_all_ref,
    own_ref, sub_ref, pooled_ref, send_ref, place_ref, tot_ref,
):
    step = pl.program_id(0)
    x = x_ref[...]
    ff = wi_ref.shape[1]
    acc = None
    for k in range(ff // chunk):
        part = slice(k * chunk, (k + 1) * chunk)
        pre_act = jnp.dot(x, wi_ref[:, part], preferred_element_type=jnp.float32) + bi_ref[:, part]
        activated = (pre_act * 0.5 * (1.0 + lax.erf(pre_act * 0.7071067811865476))).astype(
            jnp.bfloat16
        )
        term = jnp.dot(activated, wo_ref[part, :], preferred_element_type=jnp.float32)
        acc = term if acc is None else acc + term
    layer_out = (x.astype(jnp.float32) + acc + bo_ref[...]).astype(jnp.bfloat16)
    docs = tot_ref.shape[0]
    member = (
        seg_ref[...] == lax.broadcasted_iota(jnp.int32, (docs, seg_ref.shape[1]), 0)
    ).astype(jnp.bfloat16)
    part_totals = jnp.dot(member, layer_out, preferred_element_type=jnp.float32)

    @pl.when(step == 0)
    def _():
        tot_ref[...] = part_totals

    @pl.when(step != 0)
    def _():
        tot_ref[...] += part_totals

    @pl.when(step == pl.num_programs(0) - 1)
    def _():
        finish(capacity, n_owner, seg_all_ref, tot_ref, own_ref, sub_ref, pooled_ref, send_ref,
               place_ref)


def finish(capacity, n_owner, seg_ref, tot_ref, own_ref, sub_ref, pooled_ref, send_ref, place_ref):
    docs, width = tot_ref.shape
    positions = seg_ref.shape[1]
    member = seg_ref[...] == lax.broadcasted_iota(jnp.int32, (docs, positions), 0)
    counts = jnp.sum(member.astype(jnp.float32), axis=1, keepdims=True)
    mean_rows = tot_ref[...] / counts
    pooled_ref[...] = mean_rows.astype(jnp.bfloat16)
    scale_inv = lax.rsqrt(jnp.sum(mean_rows * mean_rows, axis=1, keepdims=True) + 1e-06)
    unit_rows = (mean_rows * scale_inv).astype(jnp.bfloat16)
    owner = own_ref[...]
    hits = (owner == lax.broadcasted_iota(jnp.int32, (n_owner, docs), 0)).astype(jnp.bfloat16)
    upper = (
        lax.broadcasted_iota(jnp.int32, (docs, docs), 0)
        < lax.broadcasted_iota(jnp.int32, (docs, docs), 1)
    ).astype(jnp.bfloat16)
    before = jnp.dot(hits, upper, preferred_element_type=jnp.float32)
    rank = jnp.sum(before * hits.astype(jnp.float32), axis=0, keepdims=True).astype(jnp.int32)
    place_row = owner * capacity + rank
    place_ref[...] = place_row
    slots = send_ref.shape[0]
    pick = place_row == lax.broadcasted_iota(jnp.int32, (slots, docs), 0)
    send_ref[:, :width] = jnp.dot(
        pick.astype(jnp.bfloat16), unit_rows, preferred_element_type=jnp.float32
    ).astype(jnp.bfloat16)
    key_code = sub_ref[...] + 1
    key_high = jnp.sum(jnp.where(pick, key_code // 64, 0), axis=1, keepdims=True)
    key_low = jnp.sum(jnp.where(pick, key_code % 64, 0), axis=1, keepdims=True)
    lane = lax.broadcasted_iota(jnp.int32, (slots, send_ref.shape[1] - width), 1)
    send_ref[:, width:] = jnp.where(
        lane == 0, key_high, jnp.where(lane == 1, key_low, 0)
    ).astype(jnp.bfloat16)


def encode(token_block, segments, w_in, b_in, w_out, b_out, owner_ids, sub_ids, capacity, n_owner):
    rows, width = token_block.shape
    ff = w_in.shape[1]
    docs = owner_ids.shape[0]
    slots = n_owner * capacity
    tile = 512
    flops = 4 * rows * width * ff + 2 * docs * rows * width + 2 * slots * docs * width
    whole = lambda i: (0, 0)
    return pl.pallas_call(
        functools.partial(encode_kernel, 1024, capacity, n_owner),
        out_shape=(
            jax.ShapeDtypeStruct((docs, width), jnp.bfloat16),
            jax.ShapeDtypeStruct((slots, width + 128), jnp.bfloat16),
            jax.ShapeDtypeStruct((1, docs), jnp.int32),
        ),
        grid=(rows // tile,),
        in_specs=[
            pl.BlockSpec((1, tile), lambda i: (0, i)),
            pl.BlockSpec((tile, width), lambda i: (i, 0)),
            pl.BlockSpec((width, ff), whole),
            pl.BlockSpec((1, ff), whole),
            pl.BlockSpec((ff, width), whole),
            pl.BlockSpec((1, width), whole),
            pl.BlockSpec((1, rows), whole),
            pl.BlockSpec((1, docs), whole),
            pl.BlockSpec((1, docs), whole),
        ],
        out_specs=(
            pl.BlockSpec((docs, width), whole),
            pl.BlockSpec((slots, width + 128), whole),
            pl.BlockSpec((1, docs), whole),
        ),
        scratch_shapes=[pltpu.VMEM((docs, width), jnp.float32)],
        compiler_params=pltpu.CompilerParams(
            dimension_semantics=("arbitrary",), vmem_limit_bytes=60 * 1024 * 1024
        ),
        cost_estimate=pl.CostEstimate(
            flops=flops, transcendentals=rows * ff,
            bytes_accessed=2 * rows * width + 8 * width * ff + 2 * slots * (width + 128),
        ),
    )(
        segments.reshape(1, rows), token_block, w_in, b_in.reshape(1, ff), w_out,
        b_out.reshape(1, width), segments.reshape(1, rows), owner_ids.reshape(1, docs),
        sub_ids.reshape(1, docs),
    )


def gather_grp(block):
    n = lax.axis_size("grp")
    chips = n // 2
    core_swap = [(i, i ^ 1) for i in range(n)]
    ring = [
        (i, ((i // 2 + (1 if i % 2 == 0 else chips - 1)) % chips) * 2 + i % 2) for i in range(n)
    ]
    near = lax.ppermute(block, "grp", ring)
    partner = lax.ppermute(block, "grp", core_swap)
    near_partner = lax.ppermute(partner, "grp", ring)
    far = lax.ppermute(near, "grp", ring)
    swapped = [lax.ppermute(piece, "grp", core_swap) for piece in (near, near_partner)]
    return [block, partner, near, near_partner, far] + swapped, partner, far


def per_device(tokens, segment_ids, w_in, b_in, w_out, b_out, owner_ids, sub_ids):
    n_clu = lax.axis_size("clu")
    n_grp = lax.axis_size("grp")
    doc_count = owner_ids.shape[0]
    model_width = tokens.shape[1]
    capacity = 8
    clu_index = lax.axis_index("clu")
    grp_index = lax.axis_index("grp")

    pooled, send_rows, place_row = encode(
        tokens, segment_ids[0], w_in, b_in, w_out, b_out, owner_ids, sub_ids, capacity, n_clu
    )
    slot_place = place_row[0]
    row_width = send_rows.shape[1]
    own_rows = lax.all_to_all(
        send_rows.reshape(n_clu, capacity, row_width), "clu", split_axis=0, concat_axis=0,
        tiled=True,
    ).reshape(n_clu * capacity, row_width)
    pieces, partner, far = gather_grp(own_rows)

    def key_of(rows):
        return (
            rows[:, model_width].astype(jnp.int32) * 64
            + rows[:, model_width + 1].astype(jnp.int32)
            - 1
        )

    own_key = key_of(own_rows)
    own_units = own_rows[:, :model_width]
    slots = n_clu * capacity
    best_sim = jnp.full((slots,), -1.0, jnp.float32)
    for number, piece in enumerate(pieces):
        similar = lax.dot_general(
            own_units, piece[:, :model_width], (((1,), (1,)), ((), ())),
            preferred_element_type=jnp.float32,
        )
        matched = (own_key[:, None] == key_of(piece)[None, :]) & (own_key[:, None] >= 0)
        if number == 0:
            matched = matched & (
                jnp.arange(slots, dtype=jnp.int32)[:, None]
                != jnp.arange(piece.shape[0], dtype=jnp.int32)[None, :]
            )
        best_sim = jnp.maximum(best_sim, jnp.max(jnp.where(matched, similar, -1.0), axis=1))
    partner_key = key_of(partner)
    partner_sim = lax.dot_general(
        partner[:, :model_width], far[:, :model_width], (((1,), (1,)), ((), ())),
        preferred_element_type=jnp.float32,
    )
    partner_match = (partner_key[:, None] == key_of(far)[None, :]) & (partner_key[:, None] >= 0)
    partner_best = jnp.max(jnp.where(partner_match, partner_sim, -1.0), axis=1)
    n = lax.axis_size("grp")
    best_sim = jnp.maximum(
        best_sim, lax.ppermute(partner_best, "grp", [(i, i ^ 1) for i in range(n)])
    )
    lanes = 128
    returned = lax.all_to_all(
        jnp.broadcast_to(best_sim[:, None], (slots, lanes)).reshape(n_clu, capacity, lanes),
        "clu", split_axis=0, concat_axis=0, tiled=True,
    ).reshape(slots, lanes)
    nearest = jnp.sum(
        jnp.where(
            slot_place[None, :] == jnp.arange(slots, dtype=jnp.int32)[:, None],
            returned[:, :1],
            0.0,
        ),
        axis=0,
    )
    return (pooled, nearest)


def solution(mesh):
    in_specs = (
        P(("clu", "grp"), None),
        P(("clu", "grp"), None),
        P(),
        P(),
        P(),
        P(),
        P(("clu", "grp"), None),
        P(("clu", "grp")),
    )
    out_specs = (P(("clu", "grp"), None), P(("clu", "grp")))
    return jax.shard_map(
        per_device, mesh=mesh, in_specs=in_specs, out_specs=out_specs, check_vma=False
    )
```

```python
import functools

import jax
import jax.numpy as jnp
from jax import lax
from jax.experimental import pallas as pl
from jax.experimental.pallas import tpu as pltpu
from jax.sharding import PartitionSpec as P


def encode_kernel(
    chunk, capacity, n_owner, seg_ref, x_ref, wi_ref, bi_ref, wo_hbm, bo_ref, seg_all_ref,
    own_ref, sub_ref, pooled_ref, send_ref, place_ref, tot_ref, wo_ref, wo_sem,
):
    step = pl.program_id(0)
    wo_copy = pltpu.make_async_copy(wo_hbm, wo_ref, wo_sem)

    @pl.when(step == 0)
    def _():
        wo_copy.start()

    x = x_ref[...]
    ff = wi_ref.shape[1]
    acc = None
    for k in range(ff // chunk):
        part = slice(k * chunk, (k + 1) * chunk)
        pre_act = jnp.dot(x, wi_ref[:, part], preferred_element_type=jnp.float32) + bi_ref[:, part]
        activated = (pre_act * 0.5 * (1.0 + lax.erf(pre_act * 0.7071067811865476))).astype(
            jnp.bfloat16
        )
        if k == 0:

            @pl.when(step == 0)
            def _():
                wo_copy.wait()

        term = jnp.dot(activated, wo_ref[part, :], preferred_element_type=jnp.float32)
        acc = term if acc is None else acc + term
    layer_out = (x.astype(jnp.float32) + acc + bo_ref[...]).astype(jnp.bfloat16)
    docs = tot_ref.shape[0]
    member = (
        seg_ref[...] == lax.broadcasted_iota(jnp.int32, (docs, seg_ref.shape[1]), 0)
    ).astype(jnp.bfloat16)
    part_totals = jnp.dot(member, layer_out, preferred_element_type=jnp.float32)

    @pl.when(step == 0)
    def _():
        tot_ref[...] = part_totals

    @pl.when(step != 0)
    def _():
        tot_ref[...] += part_totals

    @pl.when(step == pl.num_programs(0) - 1)
    def _():
        finish(capacity, n_owner, seg_all_ref, tot_ref, own_ref, sub_ref, pooled_ref, send_ref,
               place_ref)


def finish(capacity, n_owner, seg_ref, tot_ref, own_ref, sub_ref, pooled_ref, send_ref, place_ref):
    docs, width = tot_ref.shape
    positions = seg_ref.shape[1]
    member = seg_ref[...] == lax.broadcasted_iota(jnp.int32, (docs, positions), 0)
    counts = jnp.sum(member.astype(jnp.float32), axis=1, keepdims=True)
    mean_rows = tot_ref[...] / counts
    pooled_ref[...] = mean_rows.astype(jnp.bfloat16)
    scale_inv = lax.rsqrt(jnp.sum(mean_rows * mean_rows, axis=1, keepdims=True) + 1e-06)
    unit_rows = (mean_rows * scale_inv).astype(jnp.bfloat16)
    owner = own_ref[...]
    hits = (owner == lax.broadcasted_iota(jnp.int32, (n_owner, docs), 0)).astype(jnp.bfloat16)
    upper = (
        lax.broadcasted_iota(jnp.int32, (docs, docs), 0)
        < lax.broadcasted_iota(jnp.int32, (docs, docs), 1)
    ).astype(jnp.bfloat16)
    before = jnp.dot(hits, upper, preferred_element_type=jnp.float32)
    rank = jnp.sum(before * hits.astype(jnp.float32), axis=0, keepdims=True).astype(jnp.int32)
    place_row = owner * capacity + rank
    place_ref[...] = place_row
    slots = send_ref.shape[0]
    pick = place_row == lax.broadcasted_iota(jnp.int32, (slots, docs), 0)
    send_ref[:, :width] = jnp.dot(
        pick.astype(jnp.bfloat16), unit_rows, preferred_element_type=jnp.float32
    ).astype(jnp.bfloat16)
    key_code = sub_ref[...] + 1
    key_high = jnp.sum(jnp.where(pick, key_code // 64, 0), axis=1, keepdims=True)
    key_low = jnp.sum(jnp.where(pick, key_code % 64, 0), axis=1, keepdims=True)
    lane = lax.broadcasted_iota(jnp.int32, (slots, send_ref.shape[1] - width), 1)
    send_ref[:, width:] = jnp.where(
        lane == 0, key_high, jnp.where(lane == 1, key_low, 0)
    ).astype(jnp.bfloat16)


def encode(token_block, segments, w_in, b_in, w_out, b_out, owner_ids, sub_ids, capacity, n_owner):
    rows, width = token_block.shape
    ff = w_in.shape[1]
    docs = owner_ids.shape[0]
    slots = n_owner * capacity
    tile = 512
    flops = 4 * rows * width * ff + 2 * docs * rows * width + 2 * slots * docs * width
    whole = lambda i: (0, 0)
    return pl.pallas_call(
        functools.partial(encode_kernel, 1024, capacity, n_owner),
        out_shape=(
            jax.ShapeDtypeStruct((docs, width), jnp.bfloat16),
            jax.ShapeDtypeStruct((slots, width + 128), jnp.bfloat16),
            jax.ShapeDtypeStruct((1, docs), jnp.int32),
        ),
        grid=(rows // tile,),
        in_specs=[
            pl.BlockSpec((1, tile), lambda i: (0, i)),
            pl.BlockSpec((tile, width), lambda i: (i, 0)),
            pl.BlockSpec((width, ff), whole),
            pl.BlockSpec((1, ff), whole),
            pl.BlockSpec(memory_space=pl.ANY),
            pl.BlockSpec((1, width), whole),
            pl.BlockSpec((1, rows), whole),
            pl.BlockSpec((1, docs), whole),
            pl.BlockSpec((1, docs), whole),
        ],
        out_specs=(
            pl.BlockSpec((docs, width), whole),
            pl.BlockSpec((slots, width + 128), whole),
            pl.BlockSpec((1, docs), whole),
        ),
        scratch_shapes=[
            pltpu.VMEM((docs, width), jnp.float32),
            pltpu.VMEM((ff, width), jnp.bfloat16),
            pltpu.SemaphoreType.DMA(()),
        ],
        compiler_params=pltpu.CompilerParams(
            dimension_semantics=("arbitrary",), vmem_limit_bytes=60 * 1024 * 1024
        ),
        cost_estimate=pl.CostEstimate(
            flops=flops, transcendentals=rows * ff,
            bytes_accessed=2 * rows * width + 8 * width * ff + 2 * slots * (width + 128),
        ),
    )(
        segments.reshape(1, rows), token_block, w_in, b_in.reshape(1, ff), w_out,
        b_out.reshape(1, width), segments.reshape(1, rows), owner_ids.reshape(1, docs),
        sub_ids.reshape(1, docs),
    )


def gather_grp(block):
    n = lax.axis_size("grp")
    chips = n // 2
    core_swap = [(i, i ^ 1) for i in range(n)]
    ring = [
        (i, ((i // 2 + (1 if i % 2 == 0 else chips - 1)) % chips) * 2 + i % 2) for i in range(n)
    ]
    near = lax.ppermute(block, "grp", ring)
    partner = lax.ppermute(block, "grp", core_swap)
    near_partner = lax.ppermute(partner, "grp", ring)
    far = lax.ppermute(near, "grp", ring)
    swapped = [lax.ppermute(piece, "grp", core_swap) for piece in (near, near_partner, far)]
    return [block, partner, near, near_partner, far] + swapped


def per_device(tokens, segment_ids, w_in, b_in, w_out, b_out, owner_ids, sub_ids):
    n_clu = lax.axis_size("clu")
    n_grp = lax.axis_size("grp")
    doc_count = owner_ids.shape[0]
    model_width = tokens.shape[1]
    capacity = 8
    clu_index = lax.axis_index("clu")
    grp_index = lax.axis_index("grp")

    pooled, send_rows, place_row = encode(
        tokens, segment_ids[0], w_in, b_in, w_out, b_out, owner_ids, sub_ids, capacity, n_clu
    )
    slot_place = place_row[0]
    row_width = send_rows.shape[1]
    own_rows = lax.all_to_all(
        send_rows.reshape(n_clu, capacity, row_width), "clu", split_axis=0, concat_axis=0,
        tiled=True,
    ).reshape(n_clu * capacity, row_width)
    pieces = gather_grp(own_rows)

    def key_of(rows):
        return (
            rows[:, model_width].astype(jnp.int32) * 64
            + rows[:, model_width + 1].astype(jnp.int32)
            - 1
        )

    own_key = key_of(own_rows)
    own_units = own_rows[:, :model_width]
    slots = n_clu * capacity
    best_sim = jnp.full((slots,), -1.0, jnp.float32)
    for number, piece in enumerate(pieces):
        similar = lax.dot_general(
            own_units, piece[:, :model_width], (((1,), (1,)), ((), ())),
            preferred_element_type=jnp.float32,
        )
        matched = (own_key[:, None] == key_of(piece)[None, :]) & (own_key[:, None] >= 0)
        if number == 0:
            matched = matched & (
                jnp.arange(slots, dtype=jnp.int32)[:, None]
                != jnp.arange(piece.shape[0], dtype=jnp.int32)[None, :]
            )
        best_sim = jnp.maximum(best_sim, jnp.max(jnp.where(matched, similar, -1.0), axis=1))
    lanes = 128
    returned = lax.all_to_all(
        jnp.broadcast_to(best_sim[:, None], (slots, lanes)).reshape(n_clu, capacity, lanes),
        "clu", split_axis=0, concat_axis=0, tiled=True,
    ).reshape(slots, lanes)
    nearest = jnp.sum(
        jnp.where(
            slot_place[None, :] == jnp.arange(slots, dtype=jnp.int32)[:, None],
            returned[:, :1],
            0.0,
        ),
        axis=0,
    )
    return (pooled, nearest)


def solution(mesh):
    in_specs = (
        P(("clu", "grp"), None),
        P(("clu", "grp"), None),
        P(),
        P(),
        P(),
        P(),
        P(("clu", "grp"), None),
        P(("clu", "grp")),
    )
    out_specs = (P(("clu", "grp"), None), P(("clu", "grp")))
    return jax.shard_map(
        per_device, mesh=mesh, in_specs=in_specs, out_specs=out_specs, check_vma=False
    )
```

```python
import functools

import jax
import jax.numpy as jnp
from jax import lax
from jax.experimental import pallas as pl
from jax.experimental.pallas import tpu as pltpu
from jax.sharding import PartitionSpec as P


def encode_kernel(
    chunk, capacity, n_owner, seg_ref, x_ref, wi_ref, bi_ref, wo_ref, bo_ref, seg_all_ref,
    own_ref, sub_ref, pooled_ref, send_ref, place_ref, tot_ref,
):
    step = pl.program_id(0)
    x = x_ref[...]
    ff = wi_ref.shape[1]
    acc = None
    for k in range(ff // chunk):
        part = slice(k * chunk, (k + 1) * chunk)
        pre_act = jnp.dot(x, wi_ref[:, part], preferred_element_type=jnp.float32) + bi_ref[:, part]
        activated = (pre_act * 0.5 * (1.0 + lax.erf(pre_act * 0.7071067811865476))).astype(
            jnp.bfloat16
        )
        term = jnp.dot(activated, wo_ref[part, :], preferred_element_type=jnp.float32)
        acc = term if acc is None else acc + term
    layer_out = (x.astype(jnp.float32) + acc + bo_ref[...]).astype(jnp.bfloat16)
    docs = tot_ref.shape[0]
    member = (
        seg_ref[...] == lax.broadcasted_iota(jnp.int32, (docs, seg_ref.shape[1]), 0)
    ).astype(jnp.bfloat16)
    part_totals = jnp.dot(member, layer_out, preferred_element_type=jnp.float32)

    @pl.when(step == 0)
    def _():
        tot_ref[...] = part_totals

    @pl.when(step != 0)
    def _():
        tot_ref[...] += part_totals

    @pl.when(step == pl.num_programs(0) - 1)
    def _():
        finish(capacity, n_owner, seg_all_ref, tot_ref, own_ref, sub_ref, pooled_ref, send_ref,
               place_ref)


def finish(capacity, n_owner, seg_ref, tot_ref, own_ref, sub_ref, pooled_ref, send_ref, place_ref):
    docs, width = tot_ref.shape
    positions = seg_ref.shape[1]
    member = seg_ref[...] == lax.broadcasted_iota(jnp.int32, (docs, positions), 0)
    counts = jnp.sum(member.astype(jnp.float32), axis=1, keepdims=True)
    mean_rows = tot_ref[...] / counts
    pooled_ref[...] = mean_rows.astype(jnp.bfloat16)
    scale_inv = lax.rsqrt(jnp.sum(mean_rows * mean_rows, axis=1, keepdims=True) + 1e-06)
    unit_rows = (mean_rows * scale_inv).astype(jnp.bfloat16)
    owner = own_ref[...]
    hits = (owner == lax.broadcasted_iota(jnp.int32, (n_owner, docs), 0)).astype(jnp.bfloat16)
    upper = (
        lax.broadcasted_iota(jnp.int32, (docs, docs), 0)
        < lax.broadcasted_iota(jnp.int32, (docs, docs), 1)
    ).astype(jnp.bfloat16)
    before = jnp.dot(hits, upper, preferred_element_type=jnp.float32)
    rank = jnp.sum(before * hits.astype(jnp.float32), axis=0, keepdims=True).astype(jnp.int32)
    place_row = owner * capacity + rank
    place_ref[...] = place_row
    slots = send_ref.shape[0]
    pick = place_row == lax.broadcasted_iota(jnp.int32, (slots, docs), 0)
    send_ref[:, :width] = jnp.dot(
        pick.astype(jnp.bfloat16), unit_rows, preferred_element_type=jnp.float32
    ).astype(jnp.bfloat16)
    key_code = sub_ref[...] + 1
    key_high = jnp.sum(jnp.where(pick, key_code // 64, 0), axis=1, keepdims=True)
    key_low = jnp.sum(jnp.where(pick, key_code % 64, 0), axis=1, keepdims=True)
    lane = lax.broadcasted_iota(jnp.int32, (slots, send_ref.shape[1] - width), 1)
    send_ref[:, width:] = jnp.where(
        lane == 0, key_high, jnp.where(lane == 1, key_low, 0)
    ).astype(jnp.bfloat16)


def encode(token_block, segments, w_in, b_in, w_out, b_out, owner_ids, sub_ids, capacity, n_owner):
    rows, width = token_block.shape
    ff = w_in.shape[1]
    docs = owner_ids.shape[0]
    slots = n_owner * capacity
    tile = 512
    flops = 4 * rows * width * ff + 2 * docs * rows * width + 2 * slots * docs * width
    whole = lambda i: (0, 0)
    return pl.pallas_call(
        functools.partial(encode_kernel, 1024, capacity, n_owner),
        out_shape=(
            jax.ShapeDtypeStruct((docs, width), jnp.bfloat16),
            jax.ShapeDtypeStruct((slots, width + 128), jnp.bfloat16),
            jax.ShapeDtypeStruct((1, docs), jnp.int32),
        ),
        grid=(rows // tile,),
        in_specs=[
            pl.BlockSpec((1, tile), lambda i: (0, i)),
            pl.BlockSpec((tile, width), lambda i: (i, 0)),
            pl.BlockSpec((width, ff), whole),
            pl.BlockSpec((1, ff), whole),
            pl.BlockSpec((ff, width), whole),
            pl.BlockSpec((1, width), whole),
            pl.BlockSpec((1, rows), whole),
            pl.BlockSpec((1, docs), whole),
            pl.BlockSpec((1, docs), whole),
        ],
        out_specs=(
            pl.BlockSpec((docs, width), whole),
            pl.BlockSpec((slots, width + 128), whole),
            pl.BlockSpec((1, docs), whole),
        ),
        scratch_shapes=[pltpu.VMEM((docs, width), jnp.float32)],
        compiler_params=pltpu.CompilerParams(
            dimension_semantics=("arbitrary",), vmem_limit_bytes=60 * 1024 * 1024
        ),
        cost_estimate=pl.CostEstimate(
            flops=flops, transcendentals=rows * ff,
            bytes_accessed=2 * rows * width + 8 * width * ff + 2 * slots * (width + 128),
        ),
    )(
        segments.reshape(1, rows), token_block, w_in, b_in.reshape(1, ff), w_out,
        b_out.reshape(1, width), segments.reshape(1, rows), owner_ids.reshape(1, docs),
        sub_ids.reshape(1, docs),
    )


def gather_grp(block):
    n = lax.axis_size("grp")
    chips = n // 2
    core_swap = [(i, i ^ 1) for i in range(n)]
    ring = [
        (i, ((i // 2 + (1 if i % 2 == 0 else chips - 1)) % chips) * 2 + i % 2) for i in range(n)
    ]
    near = lax.ppermute(block, "grp", ring)
    partner = lax.ppermute(block, "grp", core_swap)
    near_partner = lax.ppermute(partner, "grp", ring)
    far = lax.ppermute(near, "grp", ring)
    swapped = [lax.ppermute(piece, "grp", core_swap) for piece in (near, near_partner, far)]
    return [block, partner, near, near_partner, far] + swapped


def per_device(tokens, segment_ids, w_in, b_in, w_out, b_out, owner_ids, sub_ids):
    n_clu = lax.axis_size("clu")
    n_grp = lax.axis_size("grp")
    doc_count = owner_ids.shape[0]
    model_width = tokens.shape[1]
    capacity = 8
    clu_index = lax.axis_index("clu")
    grp_index = lax.axis_index("grp")

    pooled, send_rows, place_row = encode(
        tokens, segment_ids[0], w_in, b_in, w_out, b_out, owner_ids, sub_ids, capacity, n_clu
    )
    slot_place = place_row[0]
    row_width = send_rows.shape[1]
    own_rows = lax.all_to_all(
        send_rows.reshape(n_clu, capacity, row_width), "clu", split_axis=0, concat_axis=0,
        tiled=True,
    ).reshape(n_clu * capacity, row_width)
    pieces = gather_grp(own_rows)

    def key_of(rows):
        return (
            rows[:, model_width].astype(jnp.int32) * 64
            + rows[:, model_width + 1].astype(jnp.int32)
            - 1
        )

    own_key = key_of(own_rows)
    own_units = own_rows[:, :model_width]
    slots = n_clu * capacity
    best_sim = jnp.full((slots,), -1.0, jnp.float32)
    for number, piece in enumerate(pieces):
        similar = lax.dot_general(
            own_units, piece[:, :model_width], (((1,), (1,)), ((), ())),
            preferred_element_type=jnp.float32,
        )
        matched = (own_key[:, None] == key_of(piece)[None, :]) & (own_key[:, None] >= 0)
        if number == 0:
            matched = matched & (
                jnp.arange(slots, dtype=jnp.int32)[:, None]
                != jnp.arange(piece.shape[0], dtype=jnp.int32)[None, :]
            )
        best_sim = jnp.maximum(best_sim, jnp.max(jnp.where(matched, similar, -1.0), axis=1))
    lanes = 128
    packed = jnp.pad(best_sim.reshape(n_clu, capacity), ((0, 0), (0, lanes - capacity)))
    returned = lax.all_to_all(
        packed.reshape(n_clu, 1, lanes), "clu", split_axis=0, concat_axis=0, tiled=True,
    ).reshape(n_clu, lanes)[:, :capacity].reshape(slots, 1)
    nearest = jnp.sum(
        jnp.where(
            slot_place[None, :] == jnp.arange(slots, dtype=jnp.int32)[:, None],
            returned,
            0.0,
        ),
        axis=0,
    )
    return (pooled, nearest)


def solution(mesh):
    in_specs = (
        P(("clu", "grp"), None),
        P(("clu", "grp"), None),
        P(),
        P(),
        P(),
        P(),
        P(("clu", "grp"), None),
        P(("clu", "grp")),
    )
    out_specs = (P(("clu", "grp"), None), P(("clu", "grp")))
    return jax.shard_map(
        per_device, mesh=mesh, in_specs=in_specs, out_specs=out_specs, check_vma=False
    )
```
